32 devices in a mesh: rep: 8 (over z, core), tp: 4 (over y, x).
Axes of the slice: x: 2, y: 2, z: 4, core: 2. Of those that a mesh axis runs over, the one named last changes fastest.
Arguments:
- partials: bfloat16 [512, 32768], P('rep', 'tp'), may hold values from -6 to 6
- residual: bfloat16 [512, 8192], P('rep', 'tp'), may hold values from -6 to 6
- lower: bfloat16 [512, 8192], P('rep', 'tp'), may hold values from -6 to 6
- middle: bfloat16 [512, 8192], P('rep', 'tp'), may hold values from -6 to 6
- accepted: int32 [256], P('rep'), may hold values from 0 to 63
- fc_weight: bfloat16 [3, 8192, 8192], P(None, 'rep', 'tp')
- norm_gain: float32 [8192], P('tp'), may hold values from 0.1 to 1.9
- grad_normed: bfloat16 [256, 8192], P('rep', 'tp')
Outputs:
- normed: bfloat16 [256, 8192], P('rep', 'tp')
- grad_fc: bfloat16 [3, 8192, 8192], P(None, 'rep', 'tp')
The draws below stay inside these ranges and needn't reach their ends.
All inputs are finite; a program needn't handle non-finite values.
Results may differ from the reference program's by a relative error of at most 0.017.
Values may be sent and summed in bfloat16 or wider, within the bound.
No kernel may reach another device: no remote copies, remote signals or barrier semaphores. Data moves between devices by JAX's collectives and lax.ppermute only.
A program may use at most 64 MiB of HBM per device.

```python
import math
import jax
import jax.numpy as jnp
from jax import lax

D = 8192
ROWS_REP = 32
CANDS = 64
ROWS = 256
CAND_TOTAL = 512
TP_WIDTH = 32768
N_TP = 4


def shared_direction(key):
    return jnp.clip(jax.random.normal(jax.random.fold_in(key, 7301), (D,), jnp.float32), -3.0, 3.0)


def draw_fc_weight(key, part):
    random_key, leading_key = jax.random.split(jax.random.fold_in(key, 7302))
    factor = 1.0 / math.sqrt(3 * D)
    random_part = jnp.clip(jax.random.normal(random_key, (3, D, D), jnp.float32), -4.0, 4.0)
    leading = jnp.clip(jax.random.normal(leading_key, (3, D, 1), jnp.float32), -3.0, 3.0)
    direction = shared_direction(key)
    values = (random_part + leading * direction[None, None, :]) * factor
    return values.astype(jnp.bfloat16)


def draw_grad_normed(key, part):
    first_key, second_key = jax.random.split(key, 2)
    row_scale = jnp.exp(jax.random.uniform(second_key, (ROWS, 1), jnp.float32, 0.0, math.log(10.0)))
    direction = shared_direction(key)[None, :]
    values = (jax.random.normal(first_key, (ROWS, D), jnp.float32) + 0.8 * direction) * row_scale
    return (values * (1.0 / math.sqrt(ROWS))).astype(jnp.bfloat16)


def plant(entries, rng, least, largest):
    place = [jax.random.randint(jax.random.fold_in(rng, axis), (), 0, length) for axis, length in enumerate(entries.shape)]
    main_axis = entries.shape.index(max(entries.shape))
    neighbour = place[:main_axis] + [(place[main_axis] + 1) % entries.shape[main_axis]] + place[main_axis + 1:]
    return entries.at[tuple(place)].set(least).at[tuple(neighbour)].set(largest)


def block_levels(key, shape, cuts, least, largest):
    level, own = 1.0, jax.random.fold_in(key, 6)
    for axis_at, shards_of in cuts:
        steps = jnp.exp(jax.random.uniform(jax.random.fold_in(own, axis_at), (shards_of,), jnp.float32, least / len(cuts), largest / len(cuts)))
        level = level * jnp.repeat(steps, shape[axis_at] // shards_of).reshape([-1 if axis == axis_at else 1 for axis in range(len(shape))])
    return level


def noise(key, dims, spread, reach, pieces=(), kind=jnp.bfloat16):
    factor_of = block_levels(key, dims, pieces, -0.22, 0.18) if pieces else 1.0
    result = jax.random.normal(key, dims, jnp.float32) * spread * factor_of
    return jnp.minimum(jnp.maximum(result, -reach), reach).astype(kind)


def setup_inputs(seed: int = 0) -> dict:
    arg_keys = jax.random.split(jax.random.key(seed), 9)
    partials = noise(arg_keys[0], (CAND_TOTAL, TP_WIDTH), 0.5, 6.0, ((0, 8), (1, 4)))
    residual = noise(arg_keys[1], (CAND_TOTAL, D), 1.0, 6.0, ((0, 8), (1, 4)))
    lower = noise(arg_keys[2], (CAND_TOTAL, D), 1.0, 6.0, ((0, 8), (1, 4)))
    middle = noise(arg_keys[3], (CAND_TOTAL, D), 1.0, 6.0, ((0, 8), (1, 4)))
    accepted = plant(jax.random.randint(arg_keys[4], (ROWS,), 0, CANDS), jax.random.fold_in(arg_keys[4], 1), 0, CANDS - 1).astype(jnp.int32)
    fc_weight = draw_fc_weight(jax.random.fold_in(arg_keys[8], 71), 0)
    norm_gain = jnp.clip(1.0 + 0.18 * jax.random.normal(arg_keys[6], (D,), jnp.float32), 0.1, 1.9)
    grad_normed = draw_grad_normed(jax.random.fold_in(arg_keys[8], 71), 0)
    return {"partials": partials, "residual": residual, "lower": lower, "middle": middle, "accepted": accepted, "fc_weight": fc_weight, "norm_gain": norm_gain, "grad_normed": grad_normed}


EPSILON = 1e-06

def reference(partials, residual, lower, middle, accepted, fc_weight, norm_gain, grad_normed):
    row_ids = jnp.arange(ROWS, dtype=jnp.int32)
    pick_rows = row_ids // ROWS_REP * CANDS + accepted.astype(jnp.int32)
    summed = lax.optimization_barrier(jnp.sum(partials[pick_rows].astype(jnp.float32).reshape(ROWS, N_TP, D), axis=1))
    upper_rows = (residual[pick_rows].astype(jnp.float32) + summed).astype(jnp.bfloat16)
    features = jnp.stack([lower[pick_rows], middle[pick_rows], upper_rows], axis=1)
    feature_flat = features.reshape(ROWS, 3 * D)
    hidden = jnp.dot(feature_flat, fc_weight.reshape(3 * D, D), preferred_element_type=jnp.float32)
    inv_rms = lax.rsqrt(lax.optimization_barrier(jnp.mean(hidden * hidden, axis=1)) + EPSILON)
    normed = (hidden * inv_rms[:, None] * norm_gain).astype(jnp.bfloat16)
    scaled = grad_normed.astype(jnp.float32) * norm_gain
    inner_sum = lax.optimization_barrier(jnp.sum(scaled * hidden, axis=1))
    grad_rows = (inv_rms[:, None] * scaled - hidden * (inv_rms ** 3 * inner_sum / D)[:, None]).astype(jnp.bfloat16)
    grad_fc = jnp.dot(feature_flat.T, grad_rows, preferred_element_type=jnp.float32).reshape(3, D, D).astype(jnp.bfloat16)
    return (normed, grad_fc)
```

```python
import jax
import jax.numpy as jnp
from jax import lax
from jax.sharding import PartitionSpec as P

D = 8192


EPSILON = 1e-06


def xor_exchange(chunk_of, axis, size):
    for k in range(1, size):
        perm = [(i, i ^ k) for i in range(size)]
        yield lax.ppermute(chunk_of(k), axis, perm)


def body(partials, residual, lower, middle, accepted, fc_weight, norm_gain, grad_normed):
    rep_count = lax.axis_size("rep")
    tp_count = lax.axis_size("tp")
    rep_index = lax.axis_index("rep")
    tp_index = lax.axis_index("tp")
    rows = accepted.shape[0]
    tp_width = residual.shape[1]

    picked = jnp.take(partials, accepted, axis=0).reshape(rows, tp_count, tp_width)
    summed = jnp.take(picked, tp_index, axis=1).astype(jnp.float32)
    for got in xor_exchange(lambda k: jnp.take(picked, tp_index ^ k, axis=1), "tp", tp_count):
        summed = summed + got.astype(jnp.float32)
    upper_rows = (jnp.take(residual, accepted, axis=0).astype(jnp.float32) + summed).astype(
        jnp.bfloat16
    )
    local_rows = jnp.stack(
        [jnp.take(lower, accepted, axis=0), jnp.take(middle, accepted, axis=0), upper_rows], axis=1
    )

    slab_width = D // rep_count
    group = rep_count // tp_count
    slabs = local_rows.reshape(rows, 3, group, slab_width)
    received = []
    for c in range(group):
        perm = []
        for r in range(rep_count):
            for t in range(tp_count):
                s = group * t + (r - c) % group
                perm.append((r * tp_count + t, s * tp_count + r // group))
        block = jnp.take(slabs, (rep_index - c) % group, axis=2)
        received.append(lax.ppermute(block, ("rep", "tp"), perm))
    stacked = jnp.stack(received, axis=0)
    order = (jnp.arange(group, dtype=jnp.int32) - rep_index) % group
    mine = jnp.take(stacked, order, axis=0).reshape(group * rows, 3, slab_width)
    features = lax.all_gather(mine, "tp", axis=0, tiled=True)

    total_rows = features.shape[0]
    feature_flat = features.reshape(total_rows, 3 * slab_width)
    fc_block = fc_weight.reshape(3 * slab_width, fc_weight.shape[2])
    hidden = lax.psum_scatter(
        jnp.dot(feature_flat, fc_block, preferred_element_type=jnp.float32),
        "rep",
        scatter_dimension=0,
        tiled=True,
    )
    squares = lax.psum(jnp.sum(hidden * hidden, axis=1), "tp")
    inv_rms = lax.rsqrt(squares / D + EPSILON)
    normed = (hidden * inv_rms[:, None] * norm_gain).astype(jnp.bfloat16)
    scaled = grad_normed.astype(jnp.float32) * norm_gain
    inner_sum = lax.psum(jnp.sum(scaled * hidden, axis=1), "tp")
    hidden_grads = (
        inv_rms[:, None] * scaled - hidden * (inv_rms**3 * inner_sum / D)[:, None]
    ).astype(jnp.bfloat16)
    hidden_grads_all = lax.all_gather(hidden_grads, "rep", axis=0, tiled=True)
    grad_fc = lax.dot_general(
        feature_flat, hidden_grads_all, (((0,), (0,)), ((), ())), preferred_element_type=jnp.float32
    )
    grad_fc = grad_fc.reshape(fc_weight.shape).astype(jnp.bfloat16)
    return (normed, grad_fc)


def solution(mesh):
    in_specs = (
        P("rep", "tp"),
        P("rep", "tp"),
        P("rep", "tp"),
        P("rep", "tp"),
        P("rep"),
        P(None, "rep", "tp"),
        P("tp"),
        P("rep", "tp"),
    )
    out_specs = (P("rep", "tp"), P(None, "rep", "tp"))
    return jax.shard_map(body, mesh=mesh, in_specs=in_specs, out_specs=out_specs, check_vma=False)
```

```python
import jax
import jax.numpy as jnp
from jax import lax
from jax.sharding import PartitionSpec as P

D = 8192


EPSILON = 1e-06


def xor_exchange(chunk_of, axis, size):
    for k in range(1, size):
        perm = [(i, i ^ k) for i in range(size)]
        yield lax.ppermute(chunk_of(k), axis, perm)


def body(partials, residual, lower, middle, accepted, fc_weight, norm_gain, grad_normed):
    rep_count = lax.axis_size("rep")
    tp_count = lax.axis_size("tp")
    rep_index = lax.axis_index("rep")
    tp_index = lax.axis_index("tp")
    rows = accepted.shape[0]
    tp_width = residual.shape[1]

    picked = jnp.take(partials, accepted, axis=0).reshape(rows, tp_count, tp_width)
    summed = jnp.take(picked, tp_index, axis=1).astype(jnp.float32)
    for got in xor_exchange(lambda k: jnp.take(picked, tp_index ^ k, axis=1), "tp", tp_count):
        summed = summed + got.astype(jnp.float32)
    upper_rows = (jnp.take(residual, accepted, axis=0).astype(jnp.float32) + summed).astype(
        jnp.bfloat16
    )
    local_rows = jnp.stack(
        [jnp.take(lower, accepted, axis=0), jnp.take(middle, accepted, axis=0), upper_rows], axis=1
    )

    slab_width = D // rep_count
    group = rep_count // tp_count
    slabs = local_rows.reshape(rows, 3, group, slab_width)
    received = []
    for c in range(group):
        perm = []
        for r in range(rep_count):
            for t in range(tp_count):
                s = group * t + (r - c) % group
                perm.append((r * tp_count + t, s * tp_count + r // group))
        block = jnp.take(slabs, (rep_index - c) % group, axis=2)
        received.append(lax.ppermute(block, ("rep", "tp"), perm))
    stacked = jnp.stack(received, axis=0)
    order = (jnp.arange(group, dtype=jnp.int32) - rep_index) % group
    mine = jnp.take(stacked, order, axis=0).reshape(group * rows, 3, slab_width)
    pieces = [mine] + list(xor_exchange(lambda k: mine, "tp", tp_count))
    source = tp_index ^ jnp.arange(tp_count, dtype=jnp.int32)
    features = jnp.take(jnp.stack(pieces, axis=0), source, axis=0)
    features = features.reshape(tp_count * group * rows, 3, slab_width)

    total_rows = features.shape[0]
    feature_flat = features.reshape(total_rows, 3 * slab_width)
    fc_block = fc_weight.reshape(3 * slab_width, fc_weight.shape[2])
    hidden = lax.psum_scatter(
        jnp.dot(feature_flat, fc_block, preferred_element_type=jnp.float32),
        "rep",
        scatter_dimension=0,
        tiled=True,
    )
    squares = lax.psum(jnp.sum(hidden * hidden, axis=1), "tp")
    inv_rms = lax.rsqrt(squares / D + EPSILON)
    normed = (hidden * inv_rms[:, None] * norm_gain).astype(jnp.bfloat16)
    scaled = grad_normed.astype(jnp.float32) * norm_gain
    inner_sum = lax.psum(jnp.sum(scaled * hidden, axis=1), "tp")
    hidden_grads = (
        inv_rms[:, None] * scaled - hidden * (inv_rms**3 * inner_sum / D)[:, None]
    ).astype(jnp.bfloat16)
    hidden_grads_all = lax.all_gather(hidden_grads, "rep", axis=0, tiled=True)
    grad_fc = lax.dot_general(
        feature_flat, hidden_grads_all, (((0,), (0,)), ((), ())), preferred_element_type=jnp.float32
    )
    grad_fc = grad_fc.reshape(fc_weight.shape).astype(jnp.bfloat16)
    return (normed, grad_fc)


def solution(mesh):
    in_specs = (
        P("rep", "tp"),
        P("rep", "tp"),
        P("rep", "tp"),
        P("rep", "tp"),
        P("rep"),
        P(None, "rep", "tp"),
        P("tp"),
        P("rep", "tp"),
    )
    out_specs = (P("rep", "tp"), P(None, "rep", "tp"))
    return jax.shard_map(body, mesh=mesh, in_specs=in_specs, out_specs=out_specs, check_vma=False)
```

```python
import jax
import jax.numpy as jnp
from jax import lax
from jax.sharding import PartitionSpec as P

D = 8192


EPSILON = 1e-06


def xor_exchange(chunk_of, axis, size):
    for k in range(1, size):
        perm = [(i, i ^ k) for i in range(size)]
        yield lax.ppermute(chunk_of(k), axis, perm)


def body(partials, residual, lower, middle, accepted, fc_weight, norm_gain, grad_normed):
    rep_count = lax.axis_size("rep")
    tp_count = lax.axis_size("tp")
    rep_index = lax.axis_index("rep")
    tp_index = lax.axis_index("tp")
    rows = accepted.shape[0]
    tp_width = residual.shape[1]

    picked = jnp.take(partials, accepted, axis=0).reshape(rows, tp_count, tp_width)
    summed = jnp.take(picked, tp_index, axis=1).astype(jnp.float32)
    for got in xor_exchange(lambda k: jnp.take(picked, tp_index ^ k, axis=1), "tp", tp_count):
        summed = summed + got.astype(jnp.float32)
    upper_rows = (jnp.take(residual, accepted, axis=0).astype(jnp.float32) + summed).astype(
        jnp.bfloat16
    )
    local_rows = jnp.stack(
        [jnp.take(lower, accepted, axis=0), jnp.take(middle, accepted, axis=0), upper_rows], axis=1
    )

    slab_width = D // rep_count
    group = rep_count // tp_count
    slabs = local_rows.reshape(rows, 3, group, slab_width)
    received = []
    for c in range(group):
        perm = []
        for r in range(rep_count):
            for t in range(tp_count):
                s = group * t + (r - c) % group
                perm.append((r * tp_count + t, s * tp_count + r // group))
        block = jnp.take(slabs, (rep_index - c) % group, axis=2)
        received.append(lax.ppermute(block, ("rep", "tp"), perm))
    stacked = jnp.stack(received, axis=0)
    order = (jnp.arange(group, dtype=jnp.int32) - rep_index) % group
    mine = jnp.take(stacked, order, axis=0).reshape(group * rows, 3, slab_width)
    pieces = [mine] + list(xor_exchange(lambda k: mine, "tp", tp_count))
    source = tp_index ^ jnp.arange(tp_count, dtype=jnp.int32)
    features = jnp.take(jnp.stack(pieces, axis=0), source, axis=0)
    features = features.reshape(tp_count * group * rows, 3, slab_width)

    total_rows = features.shape[0]
    feature_flat = features.reshape(total_rows, 3 * slab_width)
    fc_block = fc_weight.reshape(3 * slab_width, fc_weight.shape[2])
    projected = jnp.dot(feature_flat, fc_block, preferred_element_type=jnp.float32)

    parity = rep_index % 2
    chip = rep_index // 2
    by_chip = projected.reshape(rep_count // 2, 2, rows, projected.shape[1])
    own_parity = jnp.take(by_chip, parity, axis=1)
    other_parity = jnp.take(by_chip, 1 - parity, axis=1)
    chip_sum = own_parity + lax.ppermute(
        other_parity, "rep", [(i, i ^ 1) for i in range(rep_count)]
    )
    hidden = jnp.take(chip_sum, chip, axis=0)
    for k in range(1, rep_count // 2):
        block = jnp.take(chip_sum, chip ^ k, axis=0).astype(jnp.bfloat16)
        got = lax.ppermute(block, "rep", [(i, i ^ (2 * k)) for i in range(rep_count)])
        hidden = hidden + got.astype(jnp.float32)

    scaled = grad_normed.astype(jnp.float32) * norm_gain
    stats = jnp.stack([jnp.sum(hidden * hidden, axis=1), jnp.sum(scaled * hidden, axis=1)])
    gathered = jnp.stack([stats] + list(xor_exchange(lambda k: stats, "tp", tp_count)))
    stats = jnp.sum(jnp.take(gathered, tp_index ^ jnp.arange(tp_count, dtype=jnp.int32), axis=0), axis=0)
    squares, inner_sum = stats[0], stats[1]
    inv_rms = lax.rsqrt(squares / D + EPSILON)
    normed = (hidden * inv_rms[:, None] * norm_gain).astype(jnp.bfloat16)
    hidden_grads = (
        inv_rms[:, None] * scaled - hidden * (inv_rms**3 * inner_sum / D)[:, None]
    ).astype(jnp.bfloat16)
    hidden_grads_all = lax.all_gather(hidden_grads, "rep", axis=0, tiled=True)
    grad_fc = lax.dot_general(
        feature_flat, hidden_grads_all, (((0,), (0,)), ((), ())), preferred_element_type=jnp.float32
    )
    grad_fc = grad_fc.reshape(fc_weight.shape).astype(jnp.bfloat16)
    return (normed, grad_fc)


def solution(mesh):
    in_specs = (
        P("rep", "tp"),
        P("rep", "tp"),
        P("rep", "tp"),
        P("rep", "tp"),
        P("rep"),
        P(None, "rep", "tp"),
        P("tp"),
        P("rep", "tp"),
    )
    out_specs = (P("rep", "tp"), P(None, "rep", "tp"))
    return jax.shard_map(body, mesh=mesh, in_specs=in_specs, out_specs=out_specs, check_vma=False)
```

```python
import jax
import jax.numpy as jnp
from jax import lax
from jax.sharding import PartitionSpec as P

D = 8192


EPSILON = 1e-06


def xor_exchange(chunk_of, axis, size):
    for k in range(1, size):
        perm = [(i, i ^ k) for i in range(size)]
        yield lax.ppermute(chunk_of(k), axis, perm)


def pick(x, index, axis):
    return lax.dynamic_index_in_dim(x, index, axis, keepdims=False)


def place(buffer, piece, index):
    return lax.dynamic_update_index_in_dim(buffer, piece, index, 0)


def body(partials, residual, lower, middle, accepted, fc_weight, norm_gain, grad_normed):
    rep_count = lax.axis_size("rep")
    tp_count = lax.axis_size("tp")
    rep_index = lax.axis_index("rep")
    tp_index = lax.axis_index("tp")
    rows = accepted.shape[0]
    tp_width = residual.shape[1]
    parity = rep_index % 2
    chip = rep_index // 2
    chips = rep_count // 2

    picked = jnp.take(partials, accepted, axis=0).reshape(rows, tp_count, tp_width)
    summed = pick(picked, tp_index, 1).astype(jnp.float32)
    for got in xor_exchange(lambda k: pick(picked, tp_index ^ k, 1), "tp", tp_count):
        summed = summed + got.astype(jnp.float32)
    upper_rows = (jnp.take(residual, accepted, axis=0).astype(jnp.float32) + summed).astype(
        jnp.bfloat16
    )
    local_rows = jnp.stack(
        [jnp.take(lower, accepted, axis=0), jnp.take(middle, accepted, axis=0), upper_rows], axis=1
    )

    slab_width = D // rep_count
    group = rep_count // tp_count
    slabs = local_rows.reshape(rows, 3, group, slab_width)
    mine = jnp.zeros((group, rows, 3, slab_width), jnp.bfloat16)
    for c in range(group):
        perm = []
        for r in range(rep_count):
            for t in range(tp_count):
                s = group * t + (r - c) % group
                perm.append((r * tp_count + t, s * tp_count + r // group))
        block = pick(slabs, (rep_index - c) % group, 2)
        got = lax.ppermute(block, ("rep", "tp"), perm)
        mine = place(mine, got, (rep_index + c) % group)
    mine = mine.reshape(group * rows, 3, slab_width)
    features = place(jnp.zeros((tp_count,) + mine.shape, jnp.bfloat16), mine, tp_index)
    for k, got in enumerate(xor_exchange(lambda k: mine, "tp", tp_count), start=1):
        features = place(features, got, tp_index ^ k)

    total_rows = tp_count * group * rows
    feature_flat = features.reshape(total_rows, 3 * slab_width)
    fc_block = fc_weight.reshape(3 * slab_width, fc_weight.shape[2])
    projected = jnp.dot(feature_flat, fc_block, preferred_element_type=jnp.float32)

    by_chip = projected.reshape(chips, 2, rows, projected.shape[1])
    chip_sum = pick(by_chip, parity, 1) + lax.ppermute(
        pick(by_chip, 1 - parity, 1), "rep", [(i, i ^ 1) for i in range(rep_count)]
    )
    hidden = pick(chip_sum, chip, 0)
    for k in range(1, chips):
        block = pick(chip_sum, chip ^ k, 0).astype(jnp.bfloat16)
        got = lax.ppermute(block, "rep", [(i, i ^ (2 * k)) for i in range(rep_count)])
        hidden = hidden + got.astype(jnp.float32)

    scaled = grad_normed.astype(jnp.float32) * norm_gain
    stats = jnp.stack([jnp.sum(hidden * hidden, axis=1), jnp.sum(scaled * hidden, axis=1)])
    gathered = jnp.stack([stats] + list(xor_exchange(lambda k: stats, "tp", tp_count)))
    stats = jnp.sum(jnp.take(gathered, tp_index ^ jnp.arange(tp_count, dtype=jnp.int32), axis=0), axis=0)
    squares, inner_sum = stats[0], stats[1]
    inv_rms = lax.rsqrt(squares / D + EPSILON)
    normed = (hidden * inv_rms[:, None] * norm_gain).astype(jnp.bfloat16)
    hidden_grads = (
        inv_rms[:, None] * scaled - hidden * (inv_rms**3 * inner_sum / D)[:, None]
    ).astype(jnp.bfloat16)

    same_parity = place(jnp.zeros((chips,) + hidden_grads.shape, jnp.bfloat16), hidden_grads, chip)
    for k in range(1, chips):
        got = lax.ppermute(hidden_grads, "rep", [(i, i ^ (2 * k)) for i in range(rep_count)])
        same_parity = place(same_parity, got, chip ^ k)
    other_parity = lax.ppermute(same_parity, "rep", [(i, i ^ 1) for i in range(rep_count)])
    both = jnp.zeros((2, chips) + hidden_grads.shape, jnp.bfloat16)
    both = place(place(both, same_parity, parity), other_parity, 1 - parity)
    hidden_grads_all = jnp.swapaxes(both, 0, 1).reshape(rep_count * rows, hidden_grads.shape[1])

    grad_fc = lax.dot_general(
        feature_flat, hidden_grads_all, (((0,), (0,)), ((), ())), preferred_element_type=jnp.float32
    )
    grad_fc = grad_fc.reshape(fc_weight.shape).astype(jnp.bfloat16)
    return (normed, grad_fc)


def solution(mesh):
    in_specs = (
        P("rep", "tp"),
        P("rep", "tp"),
        P("rep", "tp"),
        P("rep", "tp"),
        P("rep"),
        P(None, "rep", "tp"),
        P("tp"),
        P("rep", "tp"),
    )
    out_specs = (P("rep", "tp"), P(None, "rep", "tp"))
    return jax.shard_map(body, mesh=mesh, in_specs=in_specs, out_specs=out_specs, check_vma=False)
```

```python
import jax
import jax.numpy as jnp
from jax import lax
from jax.sharding import PartitionSpec as P

D = 8192


EPSILON = 1e-06


def xor_exchange(chunk_of, axis, size):
    for k in range(1, size):
        perm = [(i, i ^ k) for i in range(size)]
        yield lax.ppermute(chunk_of(k), axis, perm)


def pick(x, index, axis):
    return lax.dynamic_index_in_dim(x, index, axis, keepdims=False)


def place(buffer, piece, index):
    return lax.dynamic_update_index_in_dim(buffer, piece, index, 0)


def body(partials, residual, lower, middle, accepted, fc_weight, norm_gain, grad_normed):
    rep_count = lax.axis_size("rep")
    tp_count = lax.axis_size("tp")
    rep_index = lax.axis_index("rep")
    tp_index = lax.axis_index("tp")
    rows = accepted.shape[0]
    tp_width = residual.shape[1]
    parity = rep_index % 2
    chip = rep_index // 2
    chips = rep_count // 2

    picked = jnp.take(partials, accepted, axis=0).reshape(rows, tp_count, tp_width)
    summed = pick(picked, tp_index, 1).astype(jnp.float32)
    for got in xor_exchange(lambda k: pick(picked, tp_index ^ k, 1), "tp", tp_count):
        summed = summed + got.astype(jnp.float32)
    upper_rows = (jnp.take(residual, accepted, axis=0).astype(jnp.float32) + summed).astype(
        jnp.bfloat16
    )

    slab_width = D // rep_count
    group = rep_count // tp_count

    def relayout(kind_rows):
        slabs = kind_rows.reshape(rows, group, slab_width)
        mine = jnp.zeros((group, rows, slab_width), jnp.bfloat16)
        for c in range(group):
            perm = []
            for r in range(rep_count):
                for t in range(tp_count):
                    s = group * t + (r - c) % group
                    perm.append((r * tp_count + t, s * tp_count + r // group))
            block = pick(slabs, (rep_index - c) % group, 1)
            got = lax.ppermute(block, ("rep", "tp"), perm)
            mine = place(mine, got, (rep_index + c) % group)
        mine = mine.reshape(group * rows, slab_width)
        gathered = place(jnp.zeros((tp_count,) + mine.shape, jnp.bfloat16), mine, tp_index)
        for k, got in enumerate(xor_exchange(lambda k: mine, "tp", tp_count), start=1):
            gathered = place(gathered, got, tp_index ^ k)
        return gathered.reshape(tp_count * group * rows, slab_width)

    kinds = [
        relayout(jnp.take(lower, accepted, axis=0)),
        relayout(jnp.take(middle, accepted, axis=0)),
        relayout(upper_rows),
    ]
    projected = jnp.dot(kinds[0], fc_weight[0], preferred_element_type=jnp.float32)
    for l in (1, 2):
        projected = projected + jnp.dot(kinds[l], fc_weight[l], preferred_element_type=jnp.float32)

    by_chip = projected.reshape(chips, 2, rows, projected.shape[1])
    chip_sum = pick(by_chip, parity, 1) + lax.ppermute(
        pick(by_chip, 1 - parity, 1), "rep", [(i, i ^ 1) for i in range(rep_count)]
    )
    hidden = pick(chip_sum, chip, 0)
    for k in range(1, chips):
        block = pick(chip_sum, chip ^ k, 0).astype(jnp.bfloat16)
        got = lax.ppermute(block, "rep", [(i, i ^ (2 * k)) for i in range(rep_count)])
        hidden = hidden + got.astype(jnp.float32)

    scaled = grad_normed.astype(jnp.float32) * norm_gain
    stats = jnp.stack([jnp.sum(hidden * hidden, axis=1), jnp.sum(scaled * hidden, axis=1)])
    gathered = jnp.stack([stats] + list(xor_exchange(lambda k: stats, "tp", tp_count)))
    stats = jnp.sum(jnp.take(gathered, tp_index ^ jnp.arange(tp_count, dtype=jnp.int32), axis=0), axis=0)
    squares, inner_sum = stats[0], stats[1]
    inv_rms = lax.rsqrt(squares / D + EPSILON)
    normed = (hidden * inv_rms[:, None] * norm_gain).astype(jnp.bfloat16)
    hidden_grads = (
        inv_rms[:, None] * scaled - hidden * (inv_rms**3 * inner_sum / D)[:, None]
    ).astype(jnp.bfloat16)

    same_parity = place(jnp.zeros((chips,) + hidden_grads.shape, jnp.bfloat16), hidden_grads, chip)
    for k in range(1, chips):
        got = lax.ppermute(hidden_grads, "rep", [(i, i ^ (2 * k)) for i in range(rep_count)])
        same_parity = place(same_parity, got, chip ^ k)
    other_parity = lax.ppermute(same_parity, "rep", [(i, i ^ 1) for i in range(rep_count)])
    both = jnp.zeros((2, chips) + hidden_grads.shape, jnp.bfloat16)
    both = place(place(both, same_parity, parity), other_parity, 1 - parity)
    hidden_grads_all = jnp.swapaxes(both, 0, 1).reshape(rep_count * rows, hidden_grads.shape[1])

    grad_fc = jnp.stack(
        [
            lax.dot_general(
                kind, hidden_grads_all, (((0,), (0,)), ((), ())), preferred_element_type=jnp.float32
            ).astype(jnp.bfloat16)
            for kind in kinds
        ]
    )
    return (normed, grad_fc)


def solution(mesh):
    in_specs = (
        P("rep", "tp"),
        P("rep", "tp"),
        P("rep", "tp"),
        P("rep", "tp"),
        P("rep"),
        P(None, "rep", "tp"),
        P("tp"),
        P("rep", "tp"),
    )
    out_specs = (P("rep", "tp"), P(None, "rep", "tp"))
    return jax.shard_map(body, mesh=mesh, in_specs=in_specs, out_specs=out_specs, check_vma=False)
```

```python
import jax
import jax.numpy as jnp
from jax import lax
from jax.sharding import PartitionSpec as P

D = 8192


EPSILON = 1e-06


def xor_exchange(chunk_of, axis, size):
    for k in range(1, size):
        perm = [(i, i ^ k) for i in range(size)]
        yield lax.ppermute(chunk_of(k), axis, perm)


def pick(x, index, axis):
    return lax.dynamic_index_in_dim(x, index, axis, keepdims=False)


def place(buffer, piece, index):
    return lax.dynamic_update_index_in_dim(buffer, piece, index, 0)


def body(partials, residual, lower, middle, accepted, fc_weight, norm_gain, grad_normed):
    rep_count = lax.axis_size("rep")
    tp_count = lax.axis_size("tp")
    rep_index = lax.axis_index("rep")
    tp_index = lax.axis_index("tp")
    rows = accepted.shape[0]
    tp_width = residual.shape[1]
    parity = rep_index % 2
    chip = rep_index // 2
    chips = rep_count // 2

    picked = jnp.take(partials, accepted, axis=0).reshape(rows, tp_count, tp_width)
    summed = pick(picked, tp_index, 1).astype(jnp.float32)
    for got in xor_exchange(lambda k: pick(picked, tp_index ^ k, 1), "tp", tp_count):
        summed = summed + got.astype(jnp.float32)
    upper_rows = (jnp.take(residual, accepted, axis=0).astype(jnp.float32) + summed).astype(
        jnp.bfloat16
    )

    slab_width = D // rep_count
    group = rep_count // tp_count

    def relayout(kind_rows):
        slabs = kind_rows.reshape(rows, group, slab_width)
        mine = jnp.zeros((group, rows, slab_width), jnp.bfloat16)
        for c in range(group):
            perm = []
            for r in range(rep_count):
                for t in range(tp_count):
                    s = group * t + (r - c) % group
                    perm.append((r * tp_count + t, s * tp_count + r // group))
            block = pick(slabs, (rep_index - c) % group, 1)
            got = lax.ppermute(block, ("rep", "tp"), perm)
            mine = place(mine, got, (rep_index + c) % group)
        mine = mine.reshape(group * rows, slab_width)
        gathered = place(jnp.zeros((tp_count,) + mine.shape, jnp.bfloat16), mine, tp_index)
        for k, got in enumerate(xor_exchange(lambda k: mine, "tp", tp_count), start=1):
            gathered = place(gathered, got, tp_index ^ k)
        return gathered.reshape(tp_count * group * rows, slab_width)

    kinds = [
        relayout(jnp.take(lower, accepted, axis=0)),
        relayout(jnp.take(middle, accepted, axis=0)),
        relayout(upper_rows),
    ]
    projected = jnp.dot(kinds[0], fc_weight[0], preferred_element_type=jnp.float32)
    for l in (1, 2):
        projected = projected + jnp.dot(kinds[l], fc_weight[l], preferred_element_type=jnp.float32)

    by_chip = projected.reshape(chips, 2, rows, projected.shape[1])
    chip_sum = pick(by_chip, parity, 1) + lax.ppermute(
        pick(by_chip, 1 - parity, 1).astype(jnp.bfloat16), "rep", [(i, i ^ 1) for i in range(rep_count)]
    ).astype(jnp.float32)
    hidden = pick(chip_sum, chip, 0)
    for k in range(1, chips):
        block = pick(chip_sum, chip ^ k, 0).astype(jnp.bfloat16)
        got = lax.ppermute(block, "rep", [(i, i ^ (2 * k)) for i in range(rep_count)])
        hidden = hidden + got.astype(jnp.float32)

    scaled = grad_normed.astype(jnp.float32) * norm_gain
    stats = jnp.stack([jnp.sum(hidden * hidden, axis=1), jnp.sum(scaled * hidden, axis=1)])
    gathered = jnp.stack([stats] + list(xor_exchange(lambda k: stats, "tp", tp_count)))
    stats = jnp.sum(jnp.take(gathered, tp_index ^ jnp.arange(tp_count, dtype=jnp.int32), axis=0), axis=0)
    squares, inner_sum = stats[0], stats[1]
    inv_rms = lax.rsqrt(squares / D + EPSILON)
    normed = (hidden * inv_rms[:, None] * norm_gain).astype(jnp.bfloat16)
    hidden_grads = (
        inv_rms[:, None] * scaled - hidden * (inv_rms**3 * inner_sum / D)[:, None]
    ).astype(jnp.bfloat16)

    same_parity = place(jnp.zeros((chips,) + hidden_grads.shape, jnp.bfloat16), hidden_grads, chip)
    for k in range(1, chips):
        got = lax.ppermute(hidden_grads, "rep", [(i, i ^ (2 * k)) for i in range(rep_count)])
        same_parity = place(same_parity, got, chip ^ k)
    other_parity = lax.ppermute(same_parity, "rep", [(i, i ^ 1) for i in range(rep_count)])
    both = jnp.zeros((2, chips) + hidden_grads.shape, jnp.bfloat16)
    both = place(place(both, same_parity, parity), other_parity, 1 - parity)
    hidden_grads_all = jnp.swapaxes(both, 0, 1).reshape(rep_count * rows, hidden_grads.shape[1])

    feature_flat = jnp.concatenate(kinds, axis=1)
    grad_fc = lax.dot_general(
        feature_flat, hidden_grads_all, (((0,), (0,)), ((), ())), preferred_element_type=jnp.float32
    )
    grad_fc = grad_fc.reshape(fc_weight.shape).astype(jnp.bfloat16)
    return (normed, grad_fc)


def solution(mesh):
    in_specs = (
        P("rep", "tp"),
        P("rep", "tp"),
        P("rep", "tp"),
        P("rep", "tp"),
        P("rep"),
        P(None, "rep", "tp"),
        P("tp"),
        P("rep", "tp"),
    )
    out_specs = (P("rep", "tp"), P(None, "rep", "tp"))
    return jax.shard_map(body, mesh=mesh, in_specs=in_specs, out_specs=out_specs, check_vma=False)
```

```python
import jax
import jax.numpy as jnp
from jax import lax
from jax.sharding import PartitionSpec as P

D = 8192


EPSILON = 1e-06


def xor_exchange(chunk_of, axis, size):
    for k in range(1, size):
        perm = [(i, i ^ k) for i in range(size)]
        yield lax.ppermute(chunk_of(k), axis, perm)


def pick(x, index, axis):
    return lax.dynamic_index_in_dim(x, index, axis, keepdims=False)


def place(buffer, piece, index):
    return lax.dynamic_update_index_in_dim(buffer, piece, index, 0)


def body(partials, residual, lower, middle, accepted, fc_weight, norm_gain, grad_normed):
    rep_count = lax.axis_size("rep")
    tp_count = lax.axis_size("tp")
    rep_index = lax.axis_index("rep")
    tp_index = lax.axis_index("tp")
    rows = accepted.shape[0]
    tp_width = residual.shape[1]
    parity = rep_index % 2
    chip = rep_index // 2
    chips = rep_count // 2

    chooser = (accepted[:, None] == jnp.arange(partials.shape[0], dtype=jnp.int32)[None, :]).astype(
        jnp.bfloat16
    )

    def take_rows(x):
        return jnp.dot(chooser, x, preferred_element_type=jnp.float32).astype(jnp.bfloat16)

    picked = take_rows(partials).reshape(rows, tp_count, tp_width)
    summed = pick(picked, tp_index, 1).astype(jnp.float32)
    for got in xor_exchange(lambda k: pick(picked, tp_index ^ k, 1), "tp", tp_count):
        summed = summed + got.astype(jnp.float32)
    upper_rows = (take_rows(residual).astype(jnp.float32) + summed).astype(
        jnp.bfloat16
    )

    slab_width = D // rep_count
    group = rep_count // tp_count

    def relayout(kind_rows):
        slabs = kind_rows.reshape(rows, group, slab_width)
        mine = jnp.zeros((group, rows, slab_width), jnp.bfloat16)
        for c in range(group):
            perm = []
            for r in range(rep_count):
                for t in range(tp_count):
                    s = group * t + (r - c) % group
                    perm.append((r * tp_count + t, s * tp_count + r // group))
            block = pick(slabs, (rep_index - c) % group, 1)
            got = lax.ppermute(block, ("rep", "tp"), perm)
            mine = place(mine, got, (rep_index + c) % group)
        mine = mine.reshape(group * rows, slab_width)
        gathered = place(jnp.zeros((tp_count,) + mine.shape, jnp.bfloat16), mine, tp_index)
        for k, got in enumerate(xor_exchange(lambda k: mine, "tp", tp_count), start=1):
            gathered = place(gathered, got, tp_index ^ k)
        return gathered.reshape(tp_count * group * rows, slab_width)

    kinds = [
        relayout(take_rows(lower)),
        relayout(take_rows(middle)),
        relayout(upper_rows),
    ]
    projected = jnp.dot(kinds[0], fc_weight[0], preferred_element_type=jnp.float32)
    for l in (1, 2):
        projected = projected + jnp.dot(kinds[l], fc_weight[l], preferred_element_type=jnp.float32)

    by_chip = projected.reshape(chips, 2, rows, projected.shape[1])
    chip_sum = pick(by_chip, parity, 1) + lax.ppermute(
        pick(by_chip, 1 - parity, 1).astype(jnp.bfloat16), "rep", [(i, i ^ 1) for i in range(rep_count)]
    ).astype(jnp.float32)
    hidden = pick(chip_sum, chip, 0)
    for k in range(1, chips):
        block = pick(chip_sum, chip ^ k, 0).astype(jnp.bfloat16)
        got = lax.ppermute(block, "rep", [(i, i ^ (2 * k)) for i in range(rep_count)])
        hidden = hidden + got.astype(jnp.float32)

    scaled = grad_normed.astype(jnp.float32) * norm_gain
    stats = jnp.stack([jnp.sum(hidden * hidden, axis=1), jnp.sum(scaled * hidden, axis=1)])
    gathered = jnp.stack([stats] + list(xor_exchange(lambda k: stats, "tp", tp_count)))
    stats = jnp.sum(jnp.take(gathered, tp_index ^ jnp.arange(tp_count, dtype=jnp.int32), axis=0), axis=0)
    squares, inner_sum = stats[0], stats[1]
    inv_rms = lax.rsqrt(squares / D + EPSILON)
    normed = (hidden * inv_rms[:, None] * norm_gain).astype(jnp.bfloat16)
    hidden_grads = (
        inv_rms[:, None] * scaled - hidden * (inv_rms**3 * inner_sum / D)[:, None]
    ).astype(jnp.bfloat16)

    same_parity = place(jnp.zeros((chips,) + hidden_grads.shape, jnp.bfloat16), hidden_grads, chip)
    for k in range(1, chips):
        got = lax.ppermute(hidden_grads, "rep", [(i, i ^ (2 * k)) for i in range(rep_count)])
        same_parity = place(same_parity, got, chip ^ k)
    other_parity = lax.ppermute(same_parity, "rep", [(i, i ^ 1) for i in range(rep_count)])
    both = jnp.zeros((2, chips) + hidden_grads.shape, jnp.bfloat16)
    both = place(place(both, same_parity, parity), other_parity, 1 - parity)
    hidden_grads_all = jnp.swapaxes(both, 0, 1).reshape(rep_count * rows, hidden_grads.shape[1])

    grad_fc = jnp.stack(
        [
            lax.dot_general(
                kind, hidden_grads_all, (((0,), (0,)), ((), ())), preferred_element_type=jnp.float32
            ).astype(jnp.bfloat16)
            for kind in kinds
        ]
    )
    return (normed, grad_fc)


def solution(mesh):
    in_specs = (
        P("rep", "tp"),
        P("rep", "tp"),
        P("rep", "tp"),
        P("rep", "tp"),
        P("rep"),
        P(None, "rep", "tp"),
        P("tp"),
        P("rep", "tp"),
    )
    out_specs = (P("rep", "tp"), P(None, "rep", "tp"))
    return jax.shard_map(body, mesh=mesh, in_specs=in_specs, out_specs=out_specs, check_vma=False)
```

```python
import jax
import jax.numpy as jnp
from jax import lax
from jax.sharding import PartitionSpec as P

D = 8192


EPSILON = 1e-06


def xor_exchange(chunk_of, axis, size):
    for k in range(1, size):
        perm = [(i, i ^ k) for i in range(size)]
        yield lax.ppermute(chunk_of(k), axis, perm)


def pick(x, index, axis):
    return lax.dynamic_index_in_dim(x, index, axis, keepdims=False)


def place(buffer, piece, index):
    return lax.dynamic_update_index_in_dim(buffer, piece, index, 0)


def body(partials, residual, lower, middle, accepted, fc_weight, norm_gain, grad_normed):
    rep_count = lax.axis_size("rep")
    tp_count = lax.axis_size("tp")
    rep_index = lax.axis_index("rep")
    tp_index = lax.axis_index("tp")
    rows = accepted.shape[0]
    tp_width = residual.shape[1]
    parity = rep_index % 2
    chip = rep_index // 2
    chips = rep_count // 2

    chooser = (accepted[:, None] == jnp.arange(partials.shape[0], dtype=jnp.int32)[None, :]).astype(
        jnp.bfloat16
    )

    def take_rows(x):
        return jnp.dot(chooser, x, preferred_element_type=jnp.float32).astype(jnp.bfloat16)

    picked = take_rows(partials).reshape(rows, tp_count, tp_width)
    summed = pick(picked, tp_index, 1).astype(jnp.float32)
    for got in xor_exchange(lambda k: pick(picked, tp_index ^ k, 1), "tp", tp_count):
        summed = summed + got.astype(jnp.float32)
    upper_rows = (take_rows(residual).astype(jnp.float32) + summed).astype(
        jnp.bfloat16
    )

    slab_width = D // rep_count
    group = rep_count // tp_count

    def relayout(kind_rows):
        slabs = kind_rows.reshape(rows, group, slab_width)
        mine = jnp.zeros((group, rows, slab_width), jnp.bfloat16)
        for c in range(group):
            perm = []
            for r in range(rep_count):
                for t in range(tp_count):
                    s = group * t + (r - c) % group
                    perm.append((r * tp_count + t, s * tp_count + r // group))
            block = pick(slabs, (rep_index - c) % group, 1)
            got = lax.ppermute(block, ("rep", "tp"), perm)
            mine = place(mine, got, (rep_index + c) % group)
        mine = mine.reshape(group * rows, slab_width)
        gathered = place(jnp.zeros((tp_count,) + mine.shape, jnp.bfloat16), mine, tp_index)
        for k, got in enumerate(xor_exchange(lambda k: mine, "tp", tp_count), start=1):
            gathered = place(gathered, got, tp_index ^ k)
        return gathered.reshape(tp_count * group * rows, slab_width)

    kinds = [
        relayout(take_rows(lower)),
        relayout(take_rows(middle)),
        relayout(upper_rows),
    ]
    projected = jnp.dot(kinds[0], fc_weight[0], preferred_element_type=jnp.float32)
    for l in (1, 2):
        projected = projected + jnp.dot(kinds[l], fc_weight[l], preferred_element_type=jnp.float32)

    by_chip = projected.reshape(chips, 2, rows, projected.shape[1])
    chip_sum = pick(by_chip, parity, 1) + lax.ppermute(
        pick(by_chip, 1 - parity, 1).astype(jnp.bfloat16), "rep", [(i, i ^ 1) for i in range(rep_count)]
    ).astype(jnp.float32)
    hidden = pick(chip_sum, chip, 0)
    for k in range(1, chips):
        block = pick(chip_sum, chip ^ k, 0).astype(jnp.bfloat16)
        got = lax.ppermute(block, "rep", [(i, i ^ (2 * k)) for i in range(rep_count)])
        hidden = hidden + got.astype(jnp.float32)

    scaled = grad_normed.astype(jnp.float32) * norm_gain
    stats = jnp.stack([jnp.sum(hidden * hidden, axis=1), jnp.sum(scaled * hidden, axis=1)])
    gathered = jnp.stack([stats] + list(xor_exchange(lambda k: stats, "tp", tp_count)))
    stats = jnp.sum(jnp.take(gathered, tp_index ^ jnp.arange(tp_count, dtype=jnp.int32), axis=0), axis=0)
    squares, inner_sum = stats[0], stats[1]
    inv_rms = lax.rsqrt(squares / D + EPSILON)
    normed = (hidden * inv_rms[:, None] * norm_gain).astype(jnp.bfloat16)
    hidden_grads = (
        inv_rms[:, None] * scaled - hidden * (inv_rms**3 * inner_sum / D)[:, None]
    ).astype(jnp.bfloat16)

    same_parity = place(jnp.zeros((chips,) + hidden_grads.shape, jnp.bfloat16), hidden_grads, chip)
    for k in range(1, chips):
        got = lax.ppermute(hidden_grads, "rep", [(i, i ^ (2 * k)) for i in range(rep_count)])
        same_parity = place(same_parity, got, chip ^ k)
    other_parity = lax.ppermute(same_parity, "rep", [(i, i ^ 1) for i in range(rep_count)])
    both = jnp.zeros((2, chips) + hidden_grads.shape, jnp.bfloat16)
    both = place(place(both, same_parity, parity), other_parity, 1 - parity)
    hidden_grads_all = jnp.swapaxes(both, 0, 1).reshape(rep_count * rows, hidden_grads.shape[1])

    stacked_kinds = jnp.stack(kinds)
    grads_per_kind = jnp.broadcast_to(hidden_grads_all, (len(kinds),) + hidden_grads_all.shape)
    grad_fc = lax.dot_general(
        stacked_kinds, grads_per_kind, (((1,), (1,)), ((0,), (0,))), preferred_element_type=jnp.float32
    ).astype(jnp.bfloat16)
    return (normed, grad_fc)


def solution(mesh):
    in_specs = (
        P("rep", "tp"),
        P("rep", "tp"),
        P("rep", "tp"),
        P("rep", "tp"),
        P("rep"),
        P(None, "rep", "tp"),
        P("tp"),
        P("rep", "tp"),
    )
    out_specs = (P("rep", "tp"), P(None, "rep", "tp"))
    return jax.shard_map(body, mesh=mesh, in_specs=in_specs, out_specs=out_specs, check_vma=False)
```

```python
import jax
import jax.numpy as jnp
from jax import lax
from jax.sharding import PartitionSpec as P


D = 8192


EPSILON = 1e-06


def xor_exchange(chunk_of, axis, size):
    for k in range(1, size):
        perm = [(i, i ^ k) for i in range(size)]
        yield lax.ppermute(chunk_of(k), axis, perm)


def pick(x, index, axis):
    return lax.dynamic_index_in_dim(x, index, axis, keepdims=False)


def place(buffer, piece, index):
    return lax.dynamic_update_index_in_dim(buffer, piece, index, 0)


def body_inner(partials, residual, lower, middle, accepted, fc_weight, norm_gain, grad_normed):
    rep_count = lax.axis_size("rep")
    tp_count = lax.axis_size("tp")
    rep_index = lax.axis_index("rep")
    tp_index = lax.axis_index("tp")
    rows = accepted.shape[0]
    tp_width = residual.shape[1]
    parity = rep_index % 2
    chip = rep_index // 2
    chips = rep_count // 2

    chooser = (accepted[:, None] == jnp.arange(partials.shape[0], dtype=jnp.int32)[None, :]).astype(
        jnp.bfloat16
    )

    def take_rows(x):
        return jnp.dot(chooser, x, preferred_element_type=jnp.float32).astype(jnp.bfloat16)

    picked = take_rows(partials).reshape(rows, tp_count, tp_width)
    summed = pick(picked, tp_index, 1).astype(jnp.float32)
    for got in xor_exchange(lambda k: pick(picked, tp_index ^ k, 1), "tp", tp_count):
        summed = summed + got.astype(jnp.float32)
    upper_rows = (take_rows(residual).astype(jnp.float32) + summed).astype(
        jnp.bfloat16
    )

    slab_width = D // rep_count
    group = rep_count // tp_count

    def relayout(kind_rows):
        return fan_out(transpose(kind_rows))

    def transpose(kind_rows):
        slabs = kind_rows.reshape(rows, group, slab_width)
        mine = jnp.zeros((group, rows, slab_width), jnp.bfloat16)
        for c in range(group):
            perm = []
            for r in range(rep_count):
                for t in range(tp_count):
                    s = group * t + (r - c) % group
                    perm.append((r * tp_count + t, s * tp_count + r // group))
            block = pick(slabs, (rep_index - c) % group, 1)
            got = lax.ppermute(block, ("rep", "tp"), perm)
            mine = place(mine, got, (rep_index + c) % group)
        return mine.reshape(group * rows, slab_width)

    def fan_out(mine):
        gathered = place(jnp.zeros((tp_count,) + mine.shape, jnp.bfloat16), mine, tp_index)
        for k, got in enumerate(xor_exchange(lambda k: mine, "tp", tp_count), start=1):
            gathered = place(gathered, got, tp_index ^ k)
        return gathered.reshape(tp_count * group * rows, slab_width)

    kinds = [relayout(take_rows(lower)), relayout(take_rows(middle)), relayout(upper_rows)]
    projected = jnp.dot(kinds[0], fc_weight[0], preferred_element_type=jnp.float32)
    for l in (1, 2):
        projected = projected + jnp.dot(kinds[l], fc_weight[l], preferred_element_type=jnp.float32)

    by_chip = projected.reshape(chips, 2, rows, projected.shape[1])
    chip_sum = pick(by_chip, parity, 1) + lax.ppermute(
        pick(by_chip, 1 - parity, 1).astype(jnp.bfloat16), "rep", [(i, i ^ 1) for i in range(rep_count)]
    ).astype(jnp.float32)
    hidden = pick(chip_sum, chip, 0)
    for k in range(1, chips):
        block = pick(chip_sum, chip ^ k, 0).astype(jnp.bfloat16)
        got = lax.ppermute(block, "rep", [(i, i ^ (2 * k)) for i in range(rep_count)])
        hidden = hidden + got.astype(jnp.float32)

    scaled = grad_normed.astype(jnp.float32) * norm_gain
    stats = jnp.stack([jnp.sum(hidden * hidden, axis=1), jnp.sum(scaled * hidden, axis=1)])
    gathered = jnp.stack([stats] + list(xor_exchange(lambda k: stats, "tp", tp_count)))
    stats = jnp.sum(jnp.take(gathered, tp_index ^ jnp.arange(tp_count, dtype=jnp.int32), axis=0), axis=0)
    squares, inner_sum = stats[0], stats[1]
    inv_rms = lax.rsqrt(squares / D + EPSILON)
    normed = (hidden * inv_rms[:, None] * norm_gain).astype(jnp.bfloat16)
    hidden_grads = (
        inv_rms[:, None] * scaled - hidden * (inv_rms**3 * inner_sum / D)[:, None]
    ).astype(jnp.bfloat16)

    same_parity = place(jnp.zeros((chips,) + hidden_grads.shape, jnp.bfloat16), hidden_grads, chip)
    for k in range(1, chips):
        got = lax.ppermute(hidden_grads, "rep", [(i, i ^ (2 * k)) for i in range(rep_count)])
        same_parity = place(same_parity, got, chip ^ k)
    other_parity = lax.ppermute(same_parity, "rep", [(i, i ^ 1) for i in range(rep_count)])
    both = jnp.zeros((2, chips) + hidden_grads.shape, jnp.bfloat16)
    both = place(place(both, same_parity, parity), other_parity, 1 - parity)
    hidden_grads_all = jnp.swapaxes(both, 0, 1).reshape(rep_count * rows, hidden_grads.shape[1])

    stacked_kinds = jnp.stack(kinds)
    grads_per_kind = jnp.broadcast_to(hidden_grads_all, (len(kinds),) + hidden_grads_all.shape)
    grad_fc = lax.dot_general(
        stacked_kinds, grads_per_kind, (((1,), (1,)), ((0,), (0,))), preferred_element_type=jnp.float32
    ).astype(jnp.bfloat16)
    return (normed, grad_fc)


def solution(mesh):
    in_specs = (
        P("rep", "tp"),
        P("rep", "tp"),
        P("rep", "tp"),
        P("rep", "tp"),
        P("rep"),
        P(None, "rep", "tp"),
        P("tp"),
        P("rep", "tp"),
    )
    out_specs = (P("rep", "tp"), P(None, "rep", "tp"))
    return jax.shard_map(body_inner, mesh=mesh, in_specs=in_specs, out_specs=out_specs, check_vma=False)
```

```python
import jax
import jax.numpy as jnp
from jax import lax
from jax.sharding import PartitionSpec as P

D = 8192


EPSILON = 1e-06


def xor_exchange(chunk_of, axis, size):
    for k in range(1, size):
        perm = [(i, i ^ k) for i in range(size)]
        yield lax.ppermute(chunk_of(k), axis, perm)


def pick(x, index, axis):
    return lax.dynamic_index_in_dim(x, index, axis, keepdims=False)


def place(buffer, piece, index):
    return lax.dynamic_update_index_in_dim(buffer, piece, index, 0)


def body(partials, residual, lower, middle, accepted, fc_weight, norm_gain, grad_normed):
    rep_count = lax.axis_size("rep")
    tp_count = lax.axis_size("tp")
    rep_index = lax.axis_index("rep")
    tp_index = lax.axis_index("tp")
    rows = accepted.shape[0]
    tp_width = residual.shape[1]
    parity = rep_index % 2
    chip = rep_index // 2
    chips = rep_count // 2

    chooser = (accepted[:, None] == jnp.arange(partials.shape[0], dtype=jnp.int32)[None, :]).astype(
        jnp.bfloat16
    )

    def take_rows(x):
        return jnp.dot(chooser, x, preferred_element_type=jnp.float32).astype(jnp.bfloat16)

    picked = take_rows(partials).reshape(rows, tp_count, tp_width)
    summed = pick(picked, tp_index, 1).astype(jnp.float32)
    for got in xor_exchange(lambda k: pick(picked, tp_index ^ k, 1), "tp", tp_count):
        summed = summed + got.astype(jnp.float32)
    upper_rows = (take_rows(residual).astype(jnp.float32) + summed).astype(
        jnp.bfloat16
    )

    slab_width = D // rep_count
    group = rep_count // tp_count

    def relayout(kind_rows):
        slabs = kind_rows.reshape(rows, group, slab_width)
        mine = jnp.zeros((group, rows, slab_width), jnp.bfloat16)
        for c in range(group):
            perm = []
            for r in range(rep_count):
                for t in range(tp_count):
                    s = group * t + (r - c) % group
                    perm.append((r * tp_count + t, s * tp_count + r // group))
            block = pick(slabs, (rep_index - c) % group, 1)
            got = lax.ppermute(block, ("rep", "tp"), perm)
            mine = place(mine, got, (rep_index + c) % group)
        mine = mine.reshape(group * rows, slab_width)
        gathered = place(jnp.zeros((tp_count,) + mine.shape, jnp.bfloat16), mine, tp_index)
        for k, got in enumerate(xor_exchange(lambda k: mine, "tp", tp_count), start=1):
            gathered = place(gathered, got, tp_index ^ k)
        return gathered.reshape(tp_count * group * rows, slab_width)

    kinds = [
        relayout(take_rows(lower)),
        relayout(take_rows(middle)),
        relayout(upper_rows),
    ]
    projected = jnp.dot(kinds[0], fc_weight[0], preferred_element_type=jnp.float32)
    for l in (1, 2):
        projected = projected + jnp.dot(kinds[l], fc_weight[l], preferred_element_type=jnp.float32)

    by_chip = projected.reshape(chips, 2, rows, projected.shape[1])
    chip_sum = pick(by_chip, parity, 1) + lax.ppermute(
        pick(by_chip, 1 - parity, 1).astype(jnp.bfloat16), "rep", [(i, i ^ 1) for i in range(rep_count)]
    ).astype(jnp.float32)
    hidden = pick(chip_sum, chip, 0)
    for k in range(1, chips):
        block = pick(chip_sum, chip ^ k, 0).astype(jnp.bfloat16)
        got = lax.ppermute(block, "rep", [(i, i ^ (2 * k)) for i in range(rep_count)])
        hidden = hidden + got.astype(jnp.float32)

    scaled = grad_normed.astype(jnp.float32) * norm_gain
    stats = jnp.stack([jnp.sum(hidden * hidden, axis=1), jnp.sum(scaled * hidden, axis=1)])
    step = 1
    while step < tp_count:
        stats = stats + lax.ppermute(stats, "tp", [(i, i ^ step) for i in range(tp_count)])
        step *= 2
    squares, inner_sum = stats[0], stats[1]
    inv_rms = lax.rsqrt(squares / D + EPSILON)
    normed = (hidden * inv_rms[:, None] * norm_gain).astype(jnp.bfloat16)
    hidden_grads = (
        inv_rms[:, None] * scaled - hidden * (inv_rms**3 * inner_sum / D)[:, None]
    ).astype(jnp.bfloat16)

    same_parity = place(jnp.zeros((chips,) + hidden_grads.shape, jnp.bfloat16), hidden_grads, chip)
    for k in range(1, chips):
        got = lax.ppermute(hidden_grads, "rep", [(i, i ^ (2 * k)) for i in range(rep_count)])
        same_parity = place(same_parity, got, chip ^ k)
    other_parity = lax.ppermute(same_parity, "rep", [(i, i ^ 1) for i in range(rep_count)])
    both = jnp.zeros((2, chips) + hidden_grads.shape, jnp.bfloat16)
    both = place(place(both, same_parity, parity), other_parity, 1 - parity)
    hidden_grads_all = jnp.swapaxes(both, 0, 1).reshape(rep_count * rows, hidden_grads.shape[1])

    stacked_kinds = jnp.stack(kinds)
    grads_per_kind = jnp.broadcast_to(hidden_grads_all, (len(kinds),) + hidden_grads_all.shape)
    grad_fc = lax.dot_general(
        stacked_kinds, grads_per_kind, (((1,), (1,)), ((0,), (0,))), preferred_element_type=jnp.float32
    ).astype(jnp.bfloat16)
    return (normed, grad_fc)


def solution(mesh):
    in_specs = (
        P("rep", "tp"),
        P("rep", "tp"),
        P("rep", "tp"),
        P("rep", "tp"),
        P("rep"),
        P(None, "rep", "tp"),
        P("tp"),
        P("rep", "tp"),
    )
    out_specs = (P("rep", "tp"), P(None, "rep", "tp"))
    return jax.shard_map(body, mesh=mesh, in_specs=in_specs, out_specs=out_specs, check_vma=False)
```

```python
import jax
import jax.numpy as jnp
from jax import lax
from jax.sharding import PartitionSpec as P

D = 8192


EPSILON = 1e-06


def xor_exchange(chunk_of, axis, size):
    for k in range(1, size):
        perm = [(i, i ^ k) for i in range(size)]
        yield lax.ppermute(chunk_of(k), axis, perm)


def pick(x, index, axis):
    return lax.dynamic_index_in_dim(x, index, axis, keepdims=False)


def place(buffer, piece, index):
    return lax.dynamic_update_index_in_dim(buffer, piece, index, 0)


def body(partials, residual, lower, middle, accepted, fc_weight, norm_gain, grad_normed):
    rep_count = lax.axis_size("rep")
    tp_count = lax.axis_size("tp")
    rep_index = lax.axis_index("rep")
    tp_index = lax.axis_index("tp")
    rows = accepted.shape[0]
    tp_width = residual.shape[1]
    parity = rep_index % 2
    chip = rep_index // 2
    chips = rep_count // 2

    chooser = (accepted[:, None] == jnp.arange(partials.shape[0], dtype=jnp.int32)[None, :]).astype(
        jnp.bfloat16
    )

    def take_rows(x):
        return jnp.dot(chooser, x, preferred_element_type=jnp.float32).astype(jnp.bfloat16)

    picked = take_rows(partials).reshape(rows, tp_count, tp_width)
    summed = pick(picked, tp_index, 1).astype(jnp.float32)
    for got in xor_exchange(lambda k: pick(picked, tp_index ^ k, 1), "tp", tp_count):
        summed = summed + got.astype(jnp.float32)
    upper_rows = (take_rows(residual).astype(jnp.float32) + summed).astype(
        jnp.bfloat16
    )

    slab_width = D // rep_count
    group = rep_count // tp_count

    def relayout(kind_rows):
        kind_count = kind_rows.shape[1]
        slabs = kind_rows.reshape(rows, kind_count, group, slab_width)
        mine = jnp.zeros((group, rows, kind_count, slab_width), jnp.bfloat16)
        for c in range(group):
            perm = []
            for r in range(rep_count):
                for t in range(tp_count):
                    s = group * t + (r - c) % group
                    perm.append((r * tp_count + t, s * tp_count + r // group))
            block = pick(slabs, (rep_index - c) % group, 2)
            got = lax.ppermute(block, ("rep", "tp"), perm)
            mine = place(mine, got, (rep_index + c) % group)
        mine = mine.reshape(group * rows, kind_count, slab_width)
        gathered = place(jnp.zeros((tp_count,) + mine.shape, jnp.bfloat16), mine, tp_index)
        for k, got in enumerate(xor_exchange(lambda k: mine, "tp", tp_count), start=1):
            gathered = place(gathered, got, tp_index ^ k)
        return gathered.reshape(tp_count * group * rows, kind_count, slab_width)

    captured = relayout(jnp.stack([take_rows(lower), take_rows(middle)], axis=1))
    joined = relayout(upper_rows[:, None, :])
    kinds = [captured[:, 0], captured[:, 1], joined[:, 0]]
    projected = jnp.dot(kinds[0], fc_weight[0], preferred_element_type=jnp.float32)
    for l in (1, 2):
        projected = projected + jnp.dot(kinds[l], fc_weight[l], preferred_element_type=jnp.float32)

    by_chip = projected.reshape(chips, 2, rows, projected.shape[1])
    chip_sum = pick(by_chip, parity, 1) + lax.ppermute(
        pick(by_chip, 1 - parity, 1).astype(jnp.bfloat16), "rep", [(i, i ^ 1) for i in range(rep_count)]
    ).astype(jnp.float32)
    hidden = pick(chip_sum, chip, 0)
    for k in range(1, chips):
        block = pick(chip_sum, chip ^ k, 0).astype(jnp.bfloat16)
        got = lax.ppermute(block, "rep", [(i, i ^ (2 * k)) for i in range(rep_count)])
        hidden = hidden + got.astype(jnp.float32)

    scaled = grad_normed.astype(jnp.float32) * norm_gain
    stats = jnp.stack([jnp.sum(hidden * hidden, axis=1), jnp.sum(scaled * hidden, axis=1)])
    step = 1
    while step < tp_count:
        stats = stats + lax.ppermute(stats, "tp", [(i, i ^ step) for i in range(tp_count)])
        step *= 2
    squares, inner_sum = stats[0], stats[1]
    inv_rms = lax.rsqrt(squares / D + EPSILON)
    normed = (hidden * inv_rms[:, None] * norm_gain).astype(jnp.bfloat16)
    hidden_grads = (
        inv_rms[:, None] * scaled - hidden * (inv_rms**3 * inner_sum / D)[:, None]
    ).astype(jnp.bfloat16)

    same_parity = place(jnp.zeros((chips,) + hidden_grads.shape, jnp.bfloat16), hidden_grads, chip)
    for k in range(1, chips):
        got = lax.ppermute(hidden_grads, "rep", [(i, i ^ (2 * k)) for i in range(rep_count)])
        same_parity = place(same_parity, got, chip ^ k)
    other_parity = lax.ppermute(same_parity, "rep", [(i, i ^ 1) for i in range(rep_count)])
    both = jnp.zeros((2, chips) + hidden_grads.shape, jnp.bfloat16)
    both = place(place(both, same_parity, parity), other_parity, 1 - parity)
    hidden_grads_all = jnp.swapaxes(both, 0, 1).reshape(rep_count * rows, hidden_grads.shape[1])

    stacked_kinds = jnp.stack(kinds)
    grads_per_kind = jnp.broadcast_to(hidden_grads_all, (len(kinds),) + hidden_grads_all.shape)
    grad_fc = lax.dot_general(
        stacked_kinds, grads_per_kind, (((1,), (1,)), ((0,), (0,))), preferred_element_type=jnp.float32
    ).astype(jnp.bfloat16)
    return (normed, grad_fc)


def solution(mesh):
    in_specs = (
        P("rep", "tp"),
        P("rep", "tp"),
        P("rep", "tp"),
        P("rep", "tp"),
        P("rep"),
        P(None, "rep", "tp"),
        P("tp"),
        P("rep", "tp"),
    )
    out_specs = (P("rep", "tp"), P(None, "rep", "tp"))
    return jax.shard_map(body, mesh=mesh, in_specs=in_specs, out_specs=out_specs, check_vma=False)
```

```python
import jax
import jax.numpy as jnp
from jax import lax
from jax.sharding import PartitionSpec as P

D = 8192


EPSILON = 1e-06


def xor_exchange(chunk_of, axis, size):
    for k in range(1, size):
        perm = [(i, i ^ k) for i in range(size)]
        yield lax.ppermute(chunk_of(k), axis, perm)


def pick(x, index, axis):
    return lax.dynamic_index_in_dim(x, index, axis, keepdims=False)


def place(buffer, piece, index):
    return lax.dynamic_update_index_in_dim(buffer, piece, index, 0)


def body(partials, residual, lower, middle, accepted, fc_weight, norm_gain, grad_normed):
    rep_count = lax.axis_size("rep")
    tp_count = lax.axis_size("tp")
    rep_index = lax.axis_index("rep")
    tp_index = lax.axis_index("tp")
    rows = accepted.shape[0]
    tp_width = residual.shape[1]
    parity = rep_index % 2
    chip = rep_index // 2
    chips = rep_count // 2

    chooser = (accepted[:, None] == jnp.arange(partials.shape[0], dtype=jnp.int32)[None, :]).astype(
        jnp.bfloat16
    )

    def take_rows(x):
        return jnp.dot(chooser, x, preferred_element_type=jnp.float32).astype(jnp.bfloat16)

    picked = take_rows(partials).reshape(rows, tp_count, tp_width)
    summed = pick(picked, tp_index, 1).astype(jnp.float32)
    for got in xor_exchange(lambda k: pick(picked, tp_index ^ k, 1), "tp", tp_count):
        summed = summed + got.astype(jnp.float32)
    upper_rows = (take_rows(residual).astype(jnp.float32) + summed).astype(
        jnp.bfloat16
    )

    slab_width = D // rep_count
    group = rep_count // tp_count

    def relayout(kind_rows):
        kind_count = kind_rows.shape[1]
        slabs = kind_rows.reshape(rows, kind_count, group, slab_width)
        mine = jnp.zeros((group, rows, kind_count, slab_width), jnp.bfloat16)
        for c in range(group):
            perm = []
            for r in range(rep_count):
                for t in range(tp_count):
                    s = group * t + (r - c) % group
                    perm.append((r * tp_count + t, s * tp_count + r // group))
            block = pick(slabs, (rep_index - c) % group, 2)
            got = lax.ppermute(block, ("rep", "tp"), perm)
            mine = place(mine, got, (rep_index + c) % group)
        mine = mine.reshape(group * rows, kind_count, slab_width)
        gathered = place(jnp.zeros((tp_count,) + mine.shape, jnp.bfloat16), mine, tp_index)
        for k, got in enumerate(xor_exchange(lambda k: mine, "tp", tp_count), start=1):
            gathered = place(gathered, got, tp_index ^ k)
        return gathered.reshape(tp_count * group * rows, kind_count, slab_width)

    captured = relayout(jnp.stack([take_rows(lower), take_rows(middle)], axis=1))
    joined = relayout(upper_rows[:, None, :])
    features = jnp.concatenate([captured, joined], axis=1)
    total_rows = features.shape[0]
    feature_flat = features.reshape(total_rows, 3 * slab_width)
    fc_block = fc_weight.reshape(3 * slab_width, fc_weight.shape[2])
    projected = jnp.dot(feature_flat, fc_block, preferred_element_type=jnp.float32)

    by_chip = projected.reshape(chips, 2, rows, projected.shape[1])
    chip_sum = pick(by_chip, parity, 1) + lax.ppermute(
        pick(by_chip, 1 - parity, 1).astype(jnp.bfloat16), "rep", [(i, i ^ 1) for i in range(rep_count)]
    ).astype(jnp.float32)
    hidden = pick(chip_sum, chip, 0)
    for k in range(1, chips):
        block = pick(chip_sum, chip ^ k, 0).astype(jnp.bfloat16)
        got = lax.ppermute(block, "rep", [(i, i ^ (2 * k)) for i in range(rep_count)])
        hidden = hidden + got.astype(jnp.float32)

    scaled = grad_normed.astype(jnp.float32) * norm_gain
    stats = jnp.stack([jnp.sum(hidden * hidden, axis=1), jnp.sum(scaled * hidden, axis=1)])
    step = 1
    while step < tp_count:
        stats = stats + lax.ppermute(stats, "tp", [(i, i ^ step) for i in range(tp_count)])
        step *= 2
    squares, inner_sum = stats[0], stats[1]
    inv_rms = lax.rsqrt(squares / D + EPSILON)
    normed = (hidden * inv_rms[:, None] * norm_gain).astype(jnp.bfloat16)
    hidden_grads = (
        inv_rms[:, None] * scaled - hidden * (inv_rms**3 * inner_sum / D)[:, None]
    ).astype(jnp.bfloat16)

    same_parity = place(jnp.zeros((chips,) + hidden_grads.shape, jnp.bfloat16), hidden_grads, chip)
    for k in range(1, chips):
        got = lax.ppermute(hidden_grads, "rep", [(i, i ^ (2 * k)) for i in range(rep_count)])
        same_parity = place(same_parity, got, chip ^ k)
    other_parity = lax.ppermute(same_parity, "rep", [(i, i ^ 1) for i in range(rep_count)])
    both = jnp.zeros((2, chips) + hidden_grads.shape, jnp.bfloat16)
    both = place(place(both, same_parity, parity), other_parity, 1 - parity)
    hidden_grads_all = jnp.swapaxes(both, 0, 1).reshape(rep_count * rows, hidden_grads.shape[1])

    grad_fc = lax.dot_general(
        feature_flat, hidden_grads_all, (((0,), (0,)), ((), ())), preferred_element_type=jnp.float32
    )
    grad_fc = grad_fc.reshape(fc_weight.shape).astype(jnp.bfloat16)
    return (normed, grad_fc)


def solution(mesh):
    in_specs = (
        P("rep", "tp"),
        P("rep", "tp"),
        P("rep", "tp"),
        P("rep", "tp"),
        P("rep"),
        P(None, "rep", "tp"),
        P("tp"),
        P("rep", "tp"),
    )
    out_specs = (P("rep", "tp"), P(None, "rep", "tp"))
    return jax.shard_map(body, mesh=mesh, in_specs=in_specs, out_specs=out_specs, check_vma=False)
```

```python
import jax
import jax.numpy as jnp
from jax import lax
from jax.sharding import PartitionSpec as P

D = 8192


EPSILON = 1e-06


def xor_exchange(chunk_of, axis, size):
    for k in range(1, size):
        perm = [(i, i ^ k) for i in range(size)]
        yield lax.ppermute(chunk_of(k), axis, perm)


def pick(x, index, axis):
    return lax.dynamic_index_in_dim(x, index, axis, keepdims=False)


def place(buffer, piece, index):
    return lax.dynamic_update_index_in_dim(buffer, piece, index, 0)


def body(partials, residual, lower, middle, accepted, fc_weight, norm_gain, grad_normed):
    rep_count = lax.axis_size("rep")
    tp_count = lax.axis_size("tp")
    rep_index = lax.axis_index("rep")
    tp_index = lax.axis_index("tp")
    rows = accepted.shape[0]
    tp_width = residual.shape[1]
    parity = rep_index % 2
    chip = rep_index // 2
    chips = rep_count // 2

    chooser = (accepted[:, None] == jnp.arange(partials.shape[0], dtype=jnp.int32)[None, :]).astype(
        jnp.bfloat16
    )

    def take_rows(x):
        return jnp.dot(chooser, x, preferred_element_type=jnp.float32).astype(jnp.bfloat16)

    picked = take_rows(partials).reshape(rows, tp_count, tp_width)
    summed = pick(picked, tp_index, 1).astype(jnp.float32)
    for got in xor_exchange(lambda k: pick(picked, tp_index ^ k, 1), "tp", tp_count):
        summed = summed + got.astype(jnp.float32)
    upper_rows = (take_rows(residual).astype(jnp.float32) + summed).astype(
        jnp.bfloat16
    )

    slab_width = D // rep_count
    group = rep_count // tp_count

    def relayout(kind_rows):
        kind_count = kind_rows.shape[1]
        slabs = kind_rows.reshape(rows, kind_count, group, slab_width)
        mine = jnp.zeros((group, rows, kind_count, slab_width), jnp.bfloat16)
        for c in range(group):
            perm = []
            for r in range(rep_count):
                for t in range(tp_count):
                    s = group * t + (r - c) % group
                    perm.append((r * tp_count + t, s * tp_count + r // group))
            block = pick(slabs, (rep_index - c) % group, 2)
            got = lax.ppermute(block, ("rep", "tp"), perm)
            mine = place(mine, got, (rep_index + c) % group)
        mine = mine.reshape(group * rows, kind_count, slab_width)
        gathered = place(jnp.zeros((tp_count,) + mine.shape, jnp.bfloat16), mine, tp_index)
        for k, got in enumerate(xor_exchange(lambda k: mine, "tp", tp_count), start=1):
            gathered = place(gathered, got, tp_index ^ k)
        return gathered.reshape(tp_count * group * rows, kind_count, slab_width)

    captured = relayout(jnp.stack([take_rows(lower), take_rows(middle)], axis=1))
    joined = relayout(upper_rows[:, None, :])
    features = jnp.concatenate([captured, joined], axis=1)
    total_rows = features.shape[0]
    feature_flat = features.reshape(total_rows, 3 * slab_width)
    fc_block = fc_weight.reshape(3 * slab_width, fc_weight.shape[2])
    projected = jnp.dot(feature_flat, fc_block, preferred_element_type=jnp.float32)

    by_chip = projected.reshape(chips, 2, rows, projected.shape[1])
    chip_sum = pick(by_chip, parity, 1) + lax.ppermute(
        pick(by_chip, 1 - parity, 1).astype(jnp.bfloat16), "rep", [(i, i ^ 1) for i in range(rep_count)]
    ).astype(jnp.float32)
    held = chip_sum
    bit = 1
    while bit < chips:
        pairs = held.reshape(held.shape[0] // 2, 2, rows, held.shape[2])
        mine_bit = (chip // bit) % 2
        sent = pick(pairs, 1 - mine_bit, 1).astype(jnp.bfloat16)
        got = lax.ppermute(sent, "rep", [(i, i ^ (2 * bit)) for i in range(rep_count)])
        held = pick(pairs, mine_bit, 1) + got.astype(jnp.float32)
        bit *= 2
    hidden = held[0]

    scaled = grad_normed.astype(jnp.float32) * norm_gain
    stats = jnp.stack([jnp.sum(hidden * hidden, axis=1), jnp.sum(scaled * hidden, axis=1)])
    step = 1
    while step < tp_count:
        stats = stats + lax.ppermute(stats, "tp", [(i, i ^ step) for i in range(tp_count)])
        step *= 2
    squares, inner_sum = stats[0], stats[1]
    inv_rms = lax.rsqrt(squares / D + EPSILON)
    normed = (hidden * inv_rms[:, None] * norm_gain).astype(jnp.bfloat16)
    hidden_grads = (
        inv_rms[:, None] * scaled - hidden * (inv_rms**3 * inner_sum / D)[:, None]
    ).astype(jnp.bfloat16)

    held = hidden_grads[None]
    bit = chips // 2
    while bit >= 1:
        got = lax.ppermute(held, "rep", [(i, i ^ (2 * bit)) for i in range(rep_count)])
        mine_bit = (chip // bit) % 2
        both = jnp.zeros((held.shape[0], 2) + hidden_grads.shape, jnp.bfloat16)
        both = lax.dynamic_update_slice_in_dim(both, held[:, None], mine_bit, 1)
        both = lax.dynamic_update_slice_in_dim(both, got[:, None], 1 - mine_bit, 1)
        held = both.reshape((2 * held.shape[0],) + hidden_grads.shape)
        bit //= 2
    other = lax.ppermute(held, "rep", [(i, i ^ 1) for i in range(rep_count)])
    both = jnp.zeros((chips, 2) + hidden_grads.shape, jnp.bfloat16)
    both = lax.dynamic_update_slice_in_dim(both, held[:, None], parity, 1)
    both = lax.dynamic_update_slice_in_dim(both, other[:, None], 1 - parity, 1)
    hidden_grads_all = both.reshape(rep_count * rows, hidden_grads.shape[1])

    grad_fc = lax.dot_general(
        feature_flat, hidden_grads_all, (((0,), (0,)), ((), ())), preferred_element_type=jnp.float32
    )
    grad_fc = grad_fc.reshape(fc_weight.shape).astype(jnp.bfloat16)
    return (normed, grad_fc)


def solution(mesh):
    in_specs = (
        P("rep", "tp"),
        P("rep", "tp"),
        P("rep", "tp"),
        P("rep", "tp"),
        P("rep"),
        P(None, "rep", "tp"),
        P("tp"),
        P("rep", "tp"),
    )
    out_specs = (P("rep", "tp"), P(None, "rep", "tp"))
    return jax.shard_map(body, mesh=mesh, in_specs=in_specs, out_specs=out_specs, check_vma=False)
```

```python
import jax
import jax.numpy as jnp
from jax import lax
from jax.sharding import PartitionSpec as P

D = 8192


EPSILON = 1e-06


def xor_exchange(chunk_of, axis, size):
    for k in range(1, size):
        perm = [(i, i ^ k) for i in range(size)]
        yield lax.ppermute(chunk_of(k), axis, perm)


def pick(x, index, axis):
    return lax.dynamic_index_in_dim(x, index, axis, keepdims=False)


def place(buffer, piece, index):
    return lax.dynamic_update_index_in_dim(buffer, piece, index, 0)


def body(partials, residual, lower, middle, accepted, fc_weight, norm_gain, grad_normed):
    rep_count = lax.axis_size("rep")
    tp_count = lax.axis_size("tp")
    rep_index = lax.axis_index("rep")
    tp_index = lax.axis_index("tp")
    rows = accepted.shape[0]
    tp_width = residual.shape[1]
    parity = rep_index % 2
    chip = rep_index // 2
    chips = rep_count // 2

    chooser = (accepted[:, None] == jnp.arange(partials.shape[0], dtype=jnp.int32)[None, :]).astype(
        jnp.bfloat16
    )

    def take_rows(x):
        return jnp.dot(chooser, x, preferred_element_type=jnp.float32).astype(jnp.bfloat16)

    picked = take_rows(partials).reshape(rows, tp_count, tp_width)
    summed = pick(picked, tp_index, 1).astype(jnp.float32)
    for got in xor_exchange(lambda k: pick(picked, tp_index ^ k, 1), "tp", tp_count):
        summed = summed + got.astype(jnp.float32)
    upper_rows = (take_rows(residual).astype(jnp.float32) + summed).astype(
        jnp.bfloat16
    )

    slab_width = D // rep_count
    group = rep_count // tp_count

    def relayout(kind_rows, features, first_kind):
        kind_count = kind_rows.shape[1]
        slabs = kind_rows.reshape(rows, kind_count, group, slab_width)
        mine = jnp.zeros((group, rows, kind_count, slab_width), jnp.bfloat16)
        for c in range(group):
            perm = []
            for r in range(rep_count):
                for t in range(tp_count):
                    s = group * t + (r - c) % group
                    perm.append((r * tp_count + t, s * tp_count + r // group))
            block = pick(slabs, (rep_index - c) % group, 2)
            got = lax.ppermute(block, ("rep", "tp"), perm)
            mine = place(mine, got, (rep_index + c) % group)
        mine = mine.reshape(group * rows, kind_count, slab_width)

        def put(features, piece, source):
            return lax.dynamic_update_slice(features, piece[None], (source, 0, first_kind, 0))

        features = put(features, mine, tp_index)
        for k, got in enumerate(xor_exchange(lambda k: mine, "tp", tp_count), start=1):
            features = put(features, got, tp_index ^ k)
        return features

    features = jnp.zeros((tp_count, group * rows, 3, slab_width), jnp.bfloat16)
    features = relayout(jnp.stack([take_rows(lower), take_rows(middle)], axis=1), features, 0)
    features = relayout(upper_rows[:, None, :], features, 2)
    features = features.reshape(tp_count * group * rows, 3, slab_width)
    total_rows = features.shape[0]
    feature_flat = features.reshape(total_rows, 3 * slab_width)
    fc_block = fc_weight.reshape(3 * slab_width, fc_weight.shape[2])
    projected = jnp.dot(feature_flat, fc_block, preferred_element_type=jnp.float32)

    by_chip = projected.reshape(chips, 2, rows, projected.shape[1])
    chip_sum = pick(by_chip, parity, 1) + lax.ppermute(
        pick(by_chip, 1 - parity, 1).astype(jnp.bfloat16), "rep", [(i, i ^ 1) for i in range(rep_count)]
    ).astype(jnp.float32)
    hidden = pick(chip_sum, chip, 0)
    for k in range(1, chips):
        block = pick(chip_sum, chip ^ k, 0).astype(jnp.bfloat16)
        got = lax.ppermute(block, "rep", [(i, i ^ (2 * k)) for i in range(rep_count)])
        hidden = hidden + got.astype(jnp.float32)

    scaled = grad_normed.astype(jnp.float32) * norm_gain
    stats = jnp.stack([jnp.sum(hidden * hidden, axis=1), jnp.sum(scaled * hidden, axis=1)])
    step = 1
    while step < tp_count:
        stats = stats + lax.ppermute(stats, "tp", [(i, i ^ step) for i in range(tp_count)])
        step *= 2
    squares, inner_sum = stats[0], stats[1]
    inv_rms = lax.rsqrt(squares / D + EPSILON)
    normed = (hidden * inv_rms[:, None] * norm_gain).astype(jnp.bfloat16)
    hidden_grads = (
        inv_rms[:, None] * scaled - hidden * (inv_rms**3 * inner_sum / D)[:, None]
    ).astype(jnp.bfloat16)

    same_parity = place(jnp.zeros((chips,) + hidden_grads.shape, jnp.bfloat16), hidden_grads, chip)
    for k in range(1, chips):
        got = lax.ppermute(hidden_grads, "rep", [(i, i ^ (2 * k)) for i in range(rep_count)])
        same_parity = place(same_parity, got, chip ^ k)
    other_parity = lax.ppermute(same_parity, "rep", [(i, i ^ 1) for i in range(rep_count)])
    both = jnp.zeros((2, chips) + hidden_grads.shape, jnp.bfloat16)
    both = place(place(both, same_parity, parity), other_parity, 1 - parity)
    hidden_grads_all = jnp.swapaxes(both, 0, 1).reshape(rep_count * rows, hidden_grads.shape[1])

    grad_fc = lax.dot_general(
        feature_flat, hidden_grads_all, (((0,), (0,)), ((), ())), preferred_element_type=jnp.float32
    )
    grad_fc = grad_fc.reshape(fc_weight.shape).astype(jnp.bfloat16)
    return (normed, grad_fc)


def solution(mesh):
    in_specs = (
        P("rep", "tp"),
        P("rep", "tp"),
        P("rep", "tp"),
        P("rep", "tp"),
        P("rep"),
        P(None, "rep", "tp"),
        P("tp"),
        P("rep", "tp"),
    )
    out_specs = (P("rep", "tp"), P(None, "rep", "tp"))
    return jax.shard_map(body, mesh=mesh, in_specs=in_specs, out_specs=out_specs, check_vma=False)
```

```python
import jax
import jax.numpy as jnp
from jax import lax
from jax.sharding import PartitionSpec as P

D = 8192


EPSILON = 1e-06


def xor_exchange(chunk_of, axis, size):
    for k in range(1, size):
        perm = [(i, i ^ k) for i in range(size)]
        yield lax.ppermute(chunk_of(k), axis, perm)


def pick(x, index, axis):
    return lax.dynamic_index_in_dim(x, index, axis, keepdims=False)


def place(buffer, piece, index):
    return lax.dynamic_update_index_in_dim(buffer, piece, index, 0)


def body(partials, residual, lower, middle, accepted, fc_weight, norm_gain, grad_normed):
    rep_count = lax.axis_size("rep")
    tp_count = lax.axis_size("tp")
    rep_index = lax.axis_index("rep")
    tp_index = lax.axis_index("tp")
    rows = accepted.shape[0]
    tp_width = residual.shape[1]
    parity = rep_index % 2
    chip = rep_index // 2
    chips = rep_count // 2

    chooser = (accepted[:, None] == jnp.arange(partials.shape[0], dtype=jnp.int32)[None, :]).astype(
        jnp.bfloat16
    )

    def take_rows(x):
        return jnp.dot(chooser, x, preferred_element_type=jnp.float32).astype(jnp.bfloat16)

    picked = take_rows(partials).reshape(rows, tp_count, tp_width)
    summed = pick(picked, tp_index, 1).astype(jnp.float32)
    for got in xor_exchange(lambda k: pick(picked, tp_index ^ k, 1), "tp", tp_count):
        summed = summed + got.astype(jnp.float32)
    upper_rows = (take_rows(residual).astype(jnp.float32) + summed).astype(
        jnp.bfloat16
    )

    slab_width = D // rep_count
    group = rep_count // tp_count

    def relayout(kind_rows):
        kind_count = kind_rows.shape[1]
        slabs = kind_rows.reshape(rows, kind_count, group, slab_width)
        mine = jnp.zeros((group, rows, kind_count, slab_width), jnp.bfloat16)
        for c in range(group):
            perm = []
            for r in range(rep_count):
                for t in range(tp_count):
                    s = group * t + (r - c) % group
                    perm.append((r * tp_count + t, s * tp_count + r // group))
            block = pick(slabs, (rep_index - c) % group, 2)
            got = lax.ppermute(block, ("rep", "tp"), perm)
            mine = place(mine, got, (rep_index + c) % group)
        mine = mine.reshape(group * rows, kind_count, slab_width)
        gathered = place(jnp.zeros((tp_count,) + mine.shape, jnp.bfloat16), mine, tp_index)
        for k, got in enumerate(xor_exchange(lambda k: mine, "tp", tp_count), start=1):
            gathered = place(gathered, got, tp_index ^ k)
        return gathered.reshape(tp_count * group * rows, kind_count, slab_width)

    captured = relayout(jnp.stack([take_rows(lower), take_rows(middle)], axis=1))
    joined = relayout(upper_rows[:, None, :])
    features = jnp.concatenate([captured, joined], axis=1)
    total_rows = features.shape[0]
    feature_flat = features.reshape(total_rows, 3 * slab_width)
    fc_block = fc_weight.reshape(3 * slab_width, fc_weight.shape[2])
    projected = jnp.dot(feature_flat, fc_block, preferred_element_type=jnp.float32)

    by_chip = projected.reshape(chips, 2, rows, projected.shape[1])
    chip_sum = pick(by_chip, parity, 1) + lax.ppermute(
        pick(by_chip, 1 - parity, 1).astype(jnp.bfloat16), "rep", [(i, i ^ 1) for i in range(rep_count)]
    ).astype(jnp.float32)
    hidden = pick(chip_sum, chip, 0)
    for k in range(1, chips):
        block = pick(chip_sum, chip ^ k, 0).astype(jnp.bfloat16)
        got = lax.ppermute(block, "rep", [(i, i ^ (2 * k)) for i in range(rep_count)])
        hidden = hidden + got.astype(jnp.float32)

    scaled = grad_normed.astype(jnp.float32) * norm_gain
    stats = jnp.stack([jnp.sum(hidden * hidden, axis=1), jnp.sum(scaled * hidden, axis=1)])
    step = 1
    while step < tp_count:
        stats = stats + lax.ppermute(stats, "tp", [(i, i ^ step) for i in range(tp_count)])
        step *= 2
    squares, inner_sum = stats[0], stats[1]
    inv_rms = lax.rsqrt(squares / D + EPSILON)
    normed = (hidden * inv_rms[:, None] * norm_gain).astype(jnp.bfloat16)
    hidden_grads = (
        inv_rms[:, None] * scaled - hidden * (inv_rms**3 * inner_sum / D)[:, None]
    ).astype(jnp.bfloat16)

    def to_sibling(piece):
        return lax.ppermute(piece, "rep", [(i, i ^ 1) for i in range(rep_count)])

    empty = jnp.zeros((chips,) + hidden_grads.shape, jnp.bfloat16)
    same_parity = place(empty, hidden_grads, chip)
    other_parity = place(empty, to_sibling(hidden_grads), chip)
    for k in range(1, chips):
        got = lax.ppermute(hidden_grads, "rep", [(i, i ^ (2 * k)) for i in range(rep_count)])
        same_parity = place(same_parity, got, chip ^ k)
        other_parity = place(other_parity, to_sibling(got), chip ^ k)
    both = jnp.zeros((2, chips) + hidden_grads.shape, jnp.bfloat16)
    both = place(place(both, same_parity, parity), other_parity, 1 - parity)
    hidden_grads_all = jnp.swapaxes(both, 0, 1).reshape(rep_count * rows, hidden_grads.shape[1])

    grad_fc = lax.dot_general(
        feature_flat, hidden_grads_all, (((0,), (0,)), ((), ())), preferred_element_type=jnp.float32
    )
    grad_fc = grad_fc.reshape(fc_weight.shape).astype(jnp.bfloat16)
    return (normed, grad_fc)


def solution(mesh):
    in_specs = (
        P("rep", "tp"),
        P("rep", "tp"),
        P("rep", "tp"),
        P("rep", "tp"),
        P("rep"),
        P(None, "rep", "tp"),
        P("tp"),
        P("rep", "tp"),
    )
    out_specs = (P("rep", "tp"), P(None, "rep", "tp"))
    return jax.shard_map(body, mesh=mesh, in_specs=in_specs, out_specs=out_specs, check_vma=False)
```

```python
import jax
import jax.numpy as jnp
from jax import lax
from jax.sharding import PartitionSpec as P

D = 8192


EPSILON = 1e-06


def xor_exchange(chunk_of, axis, size):
    for k in range(1, size):
        perm = [(i, i ^ k) for i in range(size)]
        yield lax.ppermute(chunk_of(k), axis, perm)


def pick(x, index, axis):
    return lax.dynamic_index_in_dim(x, index, axis, keepdims=False)


def place(buffer, piece, index):
    return lax.dynamic_update_index_in_dim(buffer, piece, index, 0)


def body(partials, residual, lower, middle, accepted, fc_weight, norm_gain, grad_normed):
    rep_count = lax.axis_size("rep")
    tp_count = lax.axis_size("tp")
    rep_index = lax.axis_index("rep")
    tp_index = lax.axis_index("tp")
    rows = accepted.shape[0]
    tp_width = residual.shape[1]
    parity = rep_index % 2
    chip = rep_index // 2
    chips = rep_count // 2

    chooser = (accepted[:, None] == jnp.arange(partials.shape[0], dtype=jnp.int32)[None, :]).astype(
        jnp.bfloat16
    )

    def take_rows(x):
        return jnp.dot(chooser, x, preferred_element_type=jnp.float32).astype(jnp.bfloat16)

    picked = take_rows(partials).reshape(rows, tp_count, tp_width)
    summed = pick(picked, tp_index, 1).astype(jnp.float32)
    for got in xor_exchange(lambda k: pick(picked, tp_index ^ k, 1), "tp", tp_count):
        summed = summed + got.astype(jnp.float32)
    upper_rows = (take_rows(residual).astype(jnp.float32) + summed).astype(
        jnp.bfloat16
    )

    slab_width = D // rep_count
    group = rep_count // tp_count

    def relayout(kind_rows):
        kind_count = kind_rows.shape[1]
        slabs = kind_rows.reshape(rows, kind_count, group, slab_width)
        mine = jnp.zeros((group, rows, kind_count, slab_width), jnp.bfloat16)
        for c in range(group):
            perm = []
            for r in range(rep_count):
                for t in range(tp_count):
                    s = group * t + (r - c) % group
                    perm.append((r * tp_count + t, s * tp_count + r // group))
            block = pick(slabs, (rep_index - c) % group, 2)
            got = lax.ppermute(block, ("rep", "tp"), perm)
            mine = place(mine, got, (rep_index + c) % group)
        mine = mine.reshape(group * rows, kind_count, slab_width)
        gathered = place(jnp.zeros((tp_count,) + mine.shape, jnp.bfloat16), mine, tp_index)
        for k, got in enumerate(xor_exchange(lambda k: mine, "tp", tp_count), start=1):
            gathered = place(gathered, got, tp_index ^ k)
        return gathered.reshape(tp_count * group * rows, kind_count, slab_width)

    captured = relayout(jnp.stack([take_rows(lower), take_rows(middle)], axis=1))
    joined = relayout(upper_rows[:, None, :])
    features = jnp.concatenate([captured, joined], axis=1)
    total_rows = features.shape[0]
    feature_flat = features.reshape(total_rows, 3 * slab_width)
    fc_block = fc_weight.reshape(3 * slab_width, fc_weight.shape[2])
    projected = jnp.dot(feature_flat, fc_block, preferred_element_type=jnp.float32)

    by_chip = projected.reshape(chips, 2, rows, projected.shape[1])
    own_parity = pick(by_chip, parity, 1)
    other_parity_rows = pick(by_chip, 1 - parity, 1)

    def sibling_sum(index):
        sent = pick(other_parity_rows, index, 0).astype(jnp.bfloat16)
        got = lax.ppermute(sent, "rep", [(i, i ^ 1) for i in range(rep_count)])
        return pick(own_parity, index, 0) + got.astype(jnp.float32)

    hidden = sibling_sum(chip)
    for k in range(1, chips):
        block = sibling_sum(chip ^ k).astype(jnp.bfloat16)
        got = lax.ppermute(block, "rep", [(i, i ^ (2 * k)) for i in range(rep_count)])
        hidden = hidden + got.astype(jnp.float32)

    scaled = grad_normed.astype(jnp.float32) * norm_gain
    stats = jnp.stack([jnp.sum(hidden * hidden, axis=1), jnp.sum(scaled * hidden, axis=1)])
    step = 1
    while step < tp_count:
        stats = stats + lax.ppermute(stats, "tp", [(i, i ^ step) for i in range(tp_count)])
        step *= 2
    squares, inner_sum = stats[0], stats[1]
    inv_rms = lax.rsqrt(squares / D + EPSILON)
    normed = (hidden * inv_rms[:, None] * norm_gain).astype(jnp.bfloat16)
    hidden_grads = (
        inv_rms[:, None] * scaled - hidden * (inv_rms**3 * inner_sum / D)[:, None]
    ).astype(jnp.bfloat16)

    def to_sibling(piece):
        return lax.ppermute(piece, "rep", [(i, i ^ 1) for i in range(rep_count)])

    empty = jnp.zeros((chips,) + hidden_grads.shape, jnp.bfloat16)
    same_parity = place(empty, hidden_grads, chip)
    other_parity = place(empty, to_sibling(hidden_grads), chip)
    for k in range(1, chips):
        got = lax.ppermute(hidden_grads, "rep", [(i, i ^ (2 * k)) for i in range(rep_count)])
        same_parity = place(same_parity, got, chip ^ k)
        other_parity = place(other_parity, to_sibling(got), chip ^ k)
    both = jnp.zeros((2, chips) + hidden_grads.shape, jnp.bfloat16)
    both = place(place(both, same_parity, parity), other_parity, 1 - parity)
    hidden_grads_all = jnp.swapaxes(both, 0, 1).reshape(rep_count * rows, hidden_grads.shape[1])

    grad_fc = lax.dot_general(
        feature_flat, hidden_grads_all, (((0,), (0,)), ((), ())), preferred_element_type=jnp.float32
    )
    grad_fc = grad_fc.reshape(fc_weight.shape).astype(jnp.bfloat16)
    return (normed, grad_fc)


def solution(mesh):
    in_specs = (
        P("rep", "tp"),
        P("rep", "tp"),
        P("rep", "tp"),
        P("rep", "tp"),
        P("rep"),
        P(None, "rep", "tp"),
        P("tp"),
        P("rep", "tp"),
    )
    out_specs = (P("rep", "tp"), P(None, "rep", "tp"))
    return jax.shard_map(body, mesh=mesh, in_specs=in_specs, out_specs=out_specs, check_vma=False)
```

```python
import jax
import jax.numpy as jnp
from jax import lax
from jax.sharding import PartitionSpec as P

D = 8192


EPSILON = 1e-06


def xor_exchange(chunk_of, axis, size):
    for k in range(1, size):
        perm = [(i, i ^ k) for i in range(size)]
        yield lax.ppermute(chunk_of(k), axis, perm)


def pick(x, index, axis):
    return lax.dynamic_index_in_dim(x, index, axis, keepdims=False)


def place(buffer, piece, index):
    return lax.dynamic_update_index_in_dim(buffer, piece, index, 0)


def body(partials, residual, lower, middle, accepted, fc_weight, norm_gain, grad_normed):
    rep_count = lax.axis_size("rep")
    tp_count = lax.axis_size("tp")
    rep_index = lax.axis_index("rep")
    tp_index = lax.axis_index("tp")
    rows = accepted.shape[0]
    tp_width = residual.shape[1]
    parity = rep_index % 2
    chip = rep_index // 2
    chips = rep_count // 2

    chooser = (accepted[:, None] == jnp.arange(partials.shape[0], dtype=jnp.int32)[None, :]).astype(
        jnp.bfloat16
    )

    def take_rows(x):
        return jnp.dot(chooser, x, preferred_element_type=jnp.float32).astype(jnp.bfloat16)

    picked = take_rows(partials).reshape(rows, tp_count, tp_width)
    summed = pick(picked, tp_index, 1).astype(jnp.float32)
    for got in xor_exchange(lambda k: pick(picked, tp_index ^ k, 1), "tp", tp_count):
        summed = summed + got.astype(jnp.float32)
    upper_rows = (take_rows(residual).astype(jnp.float32) + summed).astype(
        jnp.bfloat16
    )

    slab_width = D // rep_count
    group = rep_count // tp_count

    def relayout(kind_rows):
        kind_count = kind_rows.shape[1]
        slabs = kind_rows.reshape(rows, kind_count, group, slab_width)
        mine = jnp.zeros((group, rows, kind_count, slab_width), jnp.bfloat16)
        if group == 2:
            perm = [
                (r * tp_count + t, (2 * t + r % 2) * tp_count + r // 2)
                for r in range(rep_count)
                for t in range(tp_count)
            ]
            got = lax.ppermute(slabs, ("rep", "tp"), perm)
            passed = lax.ppermute(
                pick(got, 1 - parity, 2), "rep", [(i, i ^ 1) for i in range(rep_count)]
            )
            mine = place(place(mine, pick(got, parity, 2), parity), passed, 1 - parity)
        else:
            for c in range(group):
                perm = []
                for r in range(rep_count):
                    for t in range(tp_count):
                        s = group * t + (r - c) % group
                        perm.append((r * tp_count + t, s * tp_count + r // group))
                block = pick(slabs, (rep_index - c) % group, 2)
                got = lax.ppermute(block, ("rep", "tp"), perm)
                mine = place(mine, got, (rep_index + c) % group)
        mine = mine.reshape(group * rows, kind_count, slab_width)
        gathered = place(jnp.zeros((tp_count,) + mine.shape, jnp.bfloat16), mine, tp_index)
        for k, got in enumerate(xor_exchange(lambda k: mine, "tp", tp_count), start=1):
            gathered = place(gathered, got, tp_index ^ k)
        return gathered.reshape(tp_count * group * rows, kind_count, slab_width)

    captured = relayout(jnp.stack([take_rows(lower), take_rows(middle)], axis=1))
    joined = relayout(upper_rows[:, None, :])
    features = jnp.concatenate([captured, joined], axis=1)
    total_rows = features.shape[0]
    feature_flat = features.reshape(total_rows, 3 * slab_width)
    fc_block = fc_weight.reshape(3 * slab_width, fc_weight.shape[2])
    projected = jnp.dot(feature_flat, fc_block, preferred_element_type=jnp.float32)

    by_chip = projected.reshape(chips, 2, rows, projected.shape[1])
    chip_sum = pick(by_chip, parity, 1) + lax.ppermute(
        pick(by_chip, 1 - parity, 1).astype(jnp.bfloat16), "rep", [(i, i ^ 1) for i in range(rep_count)]
    ).astype(jnp.float32)
    hidden = pick(chip_sum, chip, 0)
    for k in range(1, chips):
        block = pick(chip_sum, chip ^ k, 0).astype(jnp.bfloat16)
        got = lax.ppermute(block, "rep", [(i, i ^ (2 * k)) for i in range(rep_count)])
        hidden = hidden + got.astype(jnp.float32)

    scaled = grad_normed.astype(jnp.float32) * norm_gain
    stats = jnp.stack([jnp.sum(hidden * hidden, axis=1), jnp.sum(scaled * hidden, axis=1)])
    step = 1
    while step < tp_count:
        stats = stats + lax.ppermute(stats, "tp", [(i, i ^ step) for i in range(tp_count)])
        step *= 2
    squares, inner_sum = stats[0], stats[1]
    inv_rms = lax.rsqrt(squares / D + EPSILON)
    normed = (hidden * inv_rms[:, None] * norm_gain).astype(jnp.bfloat16)
    hidden_grads = (
        inv_rms[:, None] * scaled - hidden * (inv_rms**3 * inner_sum / D)[:, None]
    ).astype(jnp.bfloat16)

    def to_sibling(piece):
        return lax.ppermute(piece, "rep", [(i, i ^ 1) for i in range(rep_count)])

    empty = jnp.zeros((chips,) + hidden_grads.shape, jnp.bfloat16)
    same_parity = place(empty, hidden_grads, chip)
    other_parity = place(empty, to_sibling(hidden_grads), chip)
    for k in range(1, chips):
        got = lax.ppermute(hidden_grads, "rep", [(i, i ^ (2 * k)) for i in range(rep_count)])
        same_parity = place(same_parity, got, chip ^ k)
        other_parity = place(other_parity, to_sibling(got), chip ^ k)
    both = jnp.zeros((2, chips) + hidden_grads.shape, jnp.bfloat16)
    both = place(place(both, same_parity, parity), other_parity, 1 - parity)
    hidden_grads_all = jnp.swapaxes(both, 0, 1).reshape(rep_count * rows, hidden_grads.shape[1])

    grad_fc = lax.dot_general(
        feature_flat, hidden_grads_all, (((0,), (0,)), ((), ())), preferred_element_type=jnp.float32
    )
    grad_fc = grad_fc.reshape(fc_weight.shape).astype(jnp.bfloat16)
    return (normed, grad_fc)


def solution(mesh):
    in_specs = (
        P("rep", "tp"),
        P("rep", "tp"),
        P("rep", "tp"),
        P("rep", "tp"),
        P("rep"),
        P(None, "rep", "tp"),
        P("tp"),
        P("rep", "tp"),
    )
    out_specs = (P("rep", "tp"), P(None, "rep", "tp"))
    return jax.shard_map(body, mesh=mesh, in_specs=in_specs, out_specs=out_specs, check_vma=False)
```

```python
import jax
import jax.numpy as jnp
from jax import lax
from jax.sharding import PartitionSpec as P

D = 8192


EPSILON = 1e-06


def xor_exchange(chunk_of, axis, size):
    for k in range(1, size):
        perm = [(i, i ^ k) for i in range(size)]
        yield lax.ppermute(chunk_of(k), axis, perm)


def pick(x, index, axis):
    return lax.dynamic_index_in_dim(x, index, axis, keepdims=False)


def place(buffer, piece, index):
    return lax.dynamic_update_index_in_dim(buffer, piece, index, 0)


def body(partials, residual, lower, middle, accepted, fc_weight, norm_gain, grad_normed):
    rep_count = lax.axis_size("rep")
    tp_count = lax.axis_size("tp")
    rep_index = lax.axis_index("rep")
    tp_index = lax.axis_index("tp")
    rows = accepted.shape[0]
    tp_width = residual.shape[1]
    parity = rep_index % 2
    chip = rep_index // 2
    chips = rep_count // 2

    chooser = (accepted[:, None] == jnp.arange(partials.shape[0], dtype=jnp.int32)[None, :]).astype(
        jnp.bfloat16
    )

    def take_rows(x):
        return jnp.dot(chooser, x, preferred_element_type=jnp.float32).astype(jnp.bfloat16)

    picked = take_rows(partials).reshape(rows, tp_count, tp_width)
    summed = pick(picked, tp_index, 1).astype(jnp.float32)
    for got in xor_exchange(lambda k: pick(picked, tp_index ^ k, 1), "tp", tp_count):
        summed = summed + got.astype(jnp.float32)
    upper_rows = (take_rows(residual).astype(jnp.float32) + summed).astype(
        jnp.bfloat16
    )

    slab_width = D // rep_count
    group = rep_count // tp_count

    def relayout(kind_list):
        width = len(kind_list) * slab_width
        split = [x.reshape(rows, group, slab_width) for x in kind_list]
        mine = jnp.zeros((group, rows, width), jnp.bfloat16)
        for c in range(group):
            perm = []
            for r in range(rep_count):
                for t in range(tp_count):
                    s = group * t + (r - c) % group
                    perm.append((r * tp_count + t, s * tp_count + r // group))
            block = jnp.concatenate([pick(x, (rep_index - c) % group, 1) for x in split], axis=1)
            got = lax.ppermute(block, ("rep", "tp"), perm)
            mine = place(mine, got, (rep_index + c) % group)
        mine = mine.reshape(group * rows, width)
        gathered = place(jnp.zeros((tp_count,) + mine.shape, jnp.bfloat16), mine, tp_index)
        for k, got in enumerate(xor_exchange(lambda k: mine, "tp", tp_count), start=1):
            gathered = place(gathered, got, tp_index ^ k)
        return gathered.reshape(tp_count * group * rows, width)

    captured = relayout([take_rows(lower), take_rows(middle)])
    joined = relayout([upper_rows])
    feature_flat = jnp.concatenate([captured, joined], axis=1)
    fc_block = fc_weight.reshape(3 * slab_width, fc_weight.shape[2])
    projected = jnp.dot(feature_flat, fc_block, preferred_element_type=jnp.float32)

    by_chip = projected.reshape(chips, 2, rows, projected.shape[1])
    chip_sum = pick(by_chip, parity, 1) + lax.ppermute(
        pick(by_chip, 1 - parity, 1).astype(jnp.bfloat16), "rep", [(i, i ^ 1) for i in range(rep_count)]
    ).astype(jnp.float32)
    hidden = pick(chip_sum, chip, 0)
    for k in range(1, chips):
        block = pick(chip_sum, chip ^ k, 0).astype(jnp.bfloat16)
        got = lax.ppermute(block, "rep", [(i, i ^ (2 * k)) for i in range(rep_count)])
        hidden = hidden + got.astype(jnp.float32)

    scaled = grad_normed.astype(jnp.float32) * norm_gain
    stats = jnp.stack([jnp.sum(hidden * hidden, axis=1), jnp.sum(scaled * hidden, axis=1)])
    step = 1
    while step < tp_count:
        stats = stats + lax.ppermute(stats, "tp", [(i, i ^ step) for i in range(tp_count)])
        step *= 2
    squares, inner_sum = stats[0], stats[1]
    inv_rms = lax.rsqrt(squares / D + EPSILON)
    normed = (hidden * inv_rms[:, None] * norm_gain).astype(jnp.bfloat16)
    hidden_grads = (
        inv_rms[:, None] * scaled - hidden * (inv_rms**3 * inner_sum / D)[:, None]
    ).astype(jnp.bfloat16)

    def to_sibling(piece):
        return lax.ppermute(piece, "rep", [(i, i ^ 1) for i in range(rep_count)])

    empty = jnp.zeros((chips,) + hidden_grads.shape, jnp.bfloat16)
    same_parity = place(empty, hidden_grads, chip)
    other_parity = place(empty, to_sibling(hidden_grads), chip)
    for k in range(1, chips):
        got = lax.ppermute(hidden_grads, "rep", [(i, i ^ (2 * k)) for i in range(rep_count)])
        same_parity = place(same_parity, got, chip ^ k)
        other_parity = place(other_parity, to_sibling(got), chip ^ k)
    both = jnp.zeros((2, chips) + hidden_grads.shape, jnp.bfloat16)
    both = place(place(both, same_parity, parity), other_parity, 1 - parity)
    hidden_grads_all = jnp.swapaxes(both, 0, 1).reshape(rep_count * rows, hidden_grads.shape[1])

    grad_fc = lax.dot_general(
        feature_flat, hidden_grads_all, (((0,), (0,)), ((), ())), preferred_element_type=jnp.float32
    )
    grad_fc = grad_fc.reshape(fc_weight.shape).astype(jnp.bfloat16)
    return (normed, grad_fc)


def solution(mesh):
    in_specs = (
        P("rep", "tp"),
        P("rep", "tp"),
        P("rep", "tp"),
        P("rep", "tp"),
        P("rep"),
        P(None, "rep", "tp"),
        P("tp"),
        P("rep", "tp"),
    )
    out_specs = (P("rep", "tp"), P(None, "rep", "tp"))
    return jax.shard_map(body, mesh=mesh, in_specs=in_specs, out_specs=out_specs, check_vma=False)
```

```python
import jax
import jax.numpy as jnp
from jax import lax
from jax.sharding import PartitionSpec as P

D = 8192


EPSILON = 1e-06


def xor_exchange(chunk_of, axis, size):
    for k in range(1, size):
        perm = [(i, i ^ k) for i in range(size)]
        yield lax.ppermute(chunk_of(k), axis, perm)


def pick(x, index, axis):
    return lax.dynamic_index_in_dim(x, index, axis, keepdims=False)


def place(buffer, piece, index):
    return lax.dynamic_update_index_in_dim(buffer, piece, index, 0)


def body(partials, residual, lower, middle, accepted, fc_weight, norm_gain, grad_normed):
    rep_count = lax.axis_size("rep")
    tp_count = lax.axis_size("tp")
    rep_index = lax.axis_index("rep")
    tp_index = lax.axis_index("tp")
    rows = accepted.shape[0]
    tp_width = residual.shape[1]
    parity = rep_index % 2
    chip = rep_index // 2
    chips = rep_count // 2

    chooser = (accepted[:, None] == jnp.arange(partials.shape[0], dtype=jnp.int32)[None, :]).astype(
        jnp.bfloat16
    )

    def take_rows(x):
        return jnp.dot(chooser, x, preferred_element_type=jnp.float32).astype(jnp.bfloat16)

    picked = take_rows(partials).reshape(rows, tp_count, tp_width)
    summed = pick(picked, tp_index, 1).astype(jnp.float32)
    for got in xor_exchange(lambda k: pick(picked, tp_index ^ k, 1), "tp", tp_count):
        summed = summed + got.astype(jnp.float32)
    upper_rows = (take_rows(residual).astype(jnp.float32) + summed).astype(
        jnp.bfloat16
    )

    slab_width = D // rep_count
    group = rep_count // tp_count

    def relayout(kind_rows):
        kind_count = kind_rows.shape[1]
        slabs = kind_rows.reshape(rows, kind_count, group, slab_width)
        mine = jnp.zeros((group, rows, kind_count, slab_width), jnp.bfloat16)
        for c in range(group):
            perm = []
            for r in range(rep_count):
                for t in range(tp_count):
                    s = group * t + (r - c) % group
                    perm.append((r * tp_count + t, s * tp_count + r // group))
            block = pick(slabs, (rep_index - c) % group, 2)
            got = lax.ppermute(block, ("rep", "tp"), perm)
            mine = place(mine, got, (rep_index + c) % group)
        mine = mine.reshape(group * rows, kind_count, slab_width)
        gathered = place(jnp.zeros((tp_count,) + mine.shape, jnp.bfloat16), mine, tp_index)
        for k, got in enumerate(xor_exchange(lambda k: mine, "tp", tp_count), start=1):
            gathered = place(gathered, got, tp_index ^ k)
        return gathered.reshape(tp_count * group * rows, kind_count, slab_width)

    captured = relayout(jnp.stack([take_rows(lower), take_rows(middle)], axis=1))
    joined = relayout(upper_rows[:, None, :])
    total_rows = captured.shape[0]
    feature_flat = jnp.concatenate(
        [captured.reshape(total_rows, -1), joined.reshape(total_rows, -1)], axis=1
    )
    fc_block = fc_weight.reshape(3 * slab_width, fc_weight.shape[2])
    projected = jnp.dot(feature_flat, fc_block, preferred_element_type=jnp.float32)

    by_chip = projected.reshape(chips, 2, rows, projected.shape[1])
    chip_sum = pick(by_chip, parity, 1) + lax.ppermute(
        pick(by_chip, 1 - parity, 1).astype(jnp.bfloat16), "rep", [(i, i ^ 1) for i in range(rep_count)]
    ).astype(jnp.float32)
    hidden = pick(chip_sum, chip, 0)
    for k in range(1, chips):
        block = pick(chip_sum, chip ^ k, 0).astype(jnp.bfloat16)
        got = lax.ppermute(block, "rep", [(i, i ^ (2 * k)) for i in range(rep_count)])
        hidden = hidden + got.astype(jnp.float32)

    scaled = grad_normed.astype(jnp.float32) * norm_gain
    stats = jnp.stack([jnp.sum(hidden * hidden, axis=1), jnp.sum(scaled * hidden, axis=1)])
    step = 1
    while step < tp_count:
        stats = stats + lax.ppermute(stats, "tp", [(i, i ^ step) for i in range(tp_count)])
        step *= 2
    squares, inner_sum = stats[0], stats[1]
    inv_rms = lax.rsqrt(squares / D + EPSILON)
    normed = (hidden * inv_rms[:, None] * norm_gain).astype(jnp.bfloat16)
    hidden_grads = (
        inv_rms[:, None] * scaled - hidden * (inv_rms**3 * inner_sum / D)[:, None]
    ).astype(jnp.bfloat16)

    def to_sibling(piece):
        return lax.ppermute(piece, "rep", [(i, i ^ 1) for i in range(rep_count)])

    empty = jnp.zeros((chips,) + hidden_grads.shape, jnp.bfloat16)
    same_parity = place(empty, hidden_grads, chip)
    other_parity = place(empty, to_sibling(hidden_grads), chip)
    for k in range(1, chips):
        got = lax.ppermute(hidden_grads, "rep", [(i, i ^ (2 * k)) for i in range(rep_count)])
        same_parity = place(same_parity, got, chip ^ k)
        other_parity = place(other_parity, to_sibling(got), chip ^ k)
    both = jnp.zeros((2, chips) + hidden_grads.shape, jnp.bfloat16)
    both = place(place(both, same_parity, parity), other_parity, 1 - parity)
    hidden_grads_all = jnp.swapaxes(both, 0, 1).reshape(rep_count * rows, hidden_grads.shape[1])

    grad_fc = lax.dot_general(
        feature_flat, hidden_grads_all, (((0,), (0,)), ((), ())), preferred_element_type=jnp.float32
    )
    grad_fc = grad_fc.reshape(fc_weight.shape).astype(jnp.bfloat16)
    return (normed, grad_fc)


def solution(mesh):
    in_specs = (
        P("rep", "tp"),
        P("rep", "tp"),
        P("rep", "tp"),
        P("rep", "tp"),
        P("rep"),
        P(None, "rep", "tp"),
        P("tp"),
        P("rep", "tp"),
    )
    out_specs = (P("rep", "tp"), P(None, "rep", "tp"))
    return jax.shard_map(body, mesh=mesh, in_specs=in_specs, out_specs=out_specs, check_vma=False)
```

```python
import jax
import jax.numpy as jnp
from jax import lax
from jax.sharding import PartitionSpec as P

D = 8192


EPSILON = 1e-06


def xor_exchange(chunk_of, axis, size):
    for k in range(1, size):
        perm = [(i, i ^ k) for i in range(size)]
        yield lax.ppermute(chunk_of(k), axis, perm)


def pick(x, index, axis):
    return lax.dynamic_index_in_dim(x, index, axis, keepdims=False)


def place(buffer, piece, index):
    return lax.dynamic_update_index_in_dim(buffer, piece, index, 0)


def body(partials, residual, lower, middle, accepted, fc_weight, norm_gain, grad_normed):
    rep_count = lax.axis_size("rep")
    tp_count = lax.axis_size("tp")
    rep_index = lax.axis_index("rep")
    tp_index = lax.axis_index("tp")
    rows = accepted.shape[0]
    tp_width = residual.shape[1]
    parity = rep_index % 2
    chip = rep_index // 2
    chips = rep_count // 2

    chooser = (accepted[:, None] == jnp.arange(partials.shape[0], dtype=jnp.int32)[None, :]).astype(
        jnp.bfloat16
    )

    def take_rows(x):
        return jnp.dot(chooser, x, preferred_element_type=jnp.float32).astype(jnp.bfloat16)

    picked = take_rows(partials).reshape(rows, tp_count, tp_width)
    summed = pick(picked, tp_index, 1).astype(jnp.float32)
    for got in xor_exchange(lambda k: pick(picked, tp_index ^ k, 1), "tp", tp_count):
        summed = summed + got.astype(jnp.float32)
    upper_rows = (take_rows(residual).astype(jnp.float32) + summed).astype(
        jnp.bfloat16
    )

    slab_width = D // rep_count
    group = rep_count // tp_count

    def relayout(kind_rows):
        kind_count = kind_rows.shape[1]
        slabs = kind_rows.reshape(rows, kind_count, group, slab_width)
        gathered = jnp.zeros((tp_count, group, rows, kind_count, slab_width), jnp.bfloat16)
        for c in range(group):
            perm = []
            for r in range(rep_count):
                for t in range(tp_count):
                    s = group * t + (r - c) % group
                    perm.append((r * tp_count + t, s * tp_count + r // group))
            block = pick(slabs, (rep_index - c) % group, 2)
            got = lax.ppermute(block, ("rep", "tp"), perm)
            spot = (rep_index + c) % group

            def put(buffer, piece, source):
                return lax.dynamic_update_slice(buffer, piece[None, None], (source, spot, 0, 0, 0))

            gathered = put(gathered, got, tp_index)
            for k, passed in enumerate(xor_exchange(lambda k: got, "tp", tp_count), start=1):
                gathered = put(gathered, passed, tp_index ^ k)
        return gathered.reshape(tp_count * group * rows, kind_count, slab_width)

    captured = relayout(jnp.stack([take_rows(lower), take_rows(middle)], axis=1))
    joined = relayout(upper_rows[:, None, :])
    features = jnp.concatenate([captured, joined], axis=1)
    total_rows = features.shape[0]
    feature_flat = features.reshape(total_rows, 3 * slab_width)
    fc_block = fc_weight.reshape(3 * slab_width, fc_weight.shape[2])
    projected = jnp.dot(feature_flat, fc_block, preferred_element_type=jnp.float32)

    by_chip = projected.reshape(chips, 2, rows, projected.shape[1])
    chip_sum = pick(by_chip, parity, 1) + lax.ppermute(
        pick(by_chip, 1 - parity, 1).astype(jnp.bfloat16), "rep", [(i, i ^ 1) for i in range(rep_count)]
    ).astype(jnp.float32)
    hidden = pick(chip_sum, chip, 0)
    for k in range(1, chips):
        block = pick(chip_sum, chip ^ k, 0).astype(jnp.bfloat16)
        got = lax.ppermute(block, "rep", [(i, i ^ (2 * k)) for i in range(rep_count)])
        hidden = hidden + got.astype(jnp.float32)

    scaled = grad_normed.astype(jnp.float32) * norm_gain
    stats = jnp.stack([jnp.sum(hidden * hidden, axis=1), jnp.sum(scaled * hidden, axis=1)])
    step = 1
    while step < tp_count:
        stats = stats + lax.ppermute(stats, "tp", [(i, i ^ step) for i in range(tp_count)])
        step *= 2
    squares, inner_sum = stats[0], stats[1]
    inv_rms = lax.rsqrt(squares / D + EPSILON)
    normed = (hidden * inv_rms[:, None] * norm_gain).astype(jnp.bfloat16)
    hidden_grads = (
        inv_rms[:, None] * scaled - hidden * (inv_rms**3 * inner_sum / D)[:, None]
    ).astype(jnp.bfloat16)

    def to_sibling(piece):
        return lax.ppermute(piece, "rep", [(i, i ^ 1) for i in range(rep_count)])

    empty = jnp.zeros((chips,) + hidden_grads.shape, jnp.bfloat16)
    same_parity = place(empty, hidden_grads, chip)
    other_parity = place(empty, to_sibling(hidden_grads), chip)
    for k in range(1, chips):
        got = lax.ppermute(hidden_grads, "rep", [(i, i ^ (2 * k)) for i in range(rep_count)])
        same_parity = place(same_parity, got, chip ^ k)
        other_parity = place(other_parity, to_sibling(got), chip ^ k)
    both = jnp.zeros((2, chips) + hidden_grads.shape, jnp.bfloat16)
    both = place(place(both, same_parity, parity), other_parity, 1 - parity)
    hidden_grads_all = jnp.swapaxes(both, 0, 1).reshape(rep_count * rows, hidden_grads.shape[1])

    grad_fc = lax.dot_general(
        feature_flat, hidden_grads_all, (((0,), (0,)), ((), ())), preferred_element_type=jnp.float32
    )
    grad_fc = grad_fc.reshape(fc_weight.shape).astype(jnp.bfloat16)
    return (normed, grad_fc)


def solution(mesh):
    in_specs = (
        P("rep", "tp"),
        P("rep", "tp"),
        P("rep", "tp"),
        P("rep", "tp"),
        P("rep"),
        P(None, "rep", "tp"),
        P("tp"),
        P("rep", "tp"),
    )
    out_specs = (P("rep", "tp"), P(None, "rep", "tp"))
    return jax.shard_map(body, mesh=mesh, in_specs=in_specs, out_specs=out_specs, check_vma=False)
```

```python
import jax
import jax.numpy as jnp
from jax import lax
from jax.sharding import PartitionSpec as P

D = 8192


EPSILON = 1e-06


def xor_exchange(chunk_of, axis, size):
    for k in range(1, size):
        perm = [(i, i ^ k) for i in range(size)]
        yield lax.ppermute(chunk_of(k), axis, perm)


def pick(x, index, axis):
    return lax.dynamic_index_in_dim(x, index, axis, keepdims=False)


def place(buffer, piece, index):
    return lax.dynamic_update_index_in_dim(buffer, piece, index, 0)


def body(partials, residual, lower, middle, accepted, fc_weight, norm_gain, grad_normed):
    rep_count = lax.axis_size("rep")
    tp_count = lax.axis_size("tp")
    rep_index = lax.axis_index("rep")
    tp_index = lax.axis_index("tp")
    rows = accepted.shape[0]
    tp_width = residual.shape[1]
    parity = rep_index % 2
    chip = rep_index // 2
    chips = rep_count // 2

    chooser = (accepted[:, None] == jnp.arange(partials.shape[0], dtype=jnp.int32)[None, :]).astype(
        jnp.bfloat16
    )

    def take_rows(x):
        return jnp.dot(chooser, x, preferred_element_type=jnp.float32).astype(jnp.bfloat16)

    picked = take_rows(partials).reshape(rows, tp_count, tp_width)
    summed = pick(picked, tp_index, 1).astype(jnp.float32)
    for got in xor_exchange(lambda k: pick(picked, tp_index ^ k, 1), "tp", tp_count):
        summed = summed + got.astype(jnp.float32)
    upper_rows = (take_rows(residual).astype(jnp.float32) + summed).astype(
        jnp.bfloat16
    )

    slab_width = D // rep_count
    group = rep_count // tp_count

    def relayout(kind_rows):
        kind_count = kind_rows.shape[1]
        slabs = kind_rows.reshape(rows, kind_count, group, slab_width)
        gathered = jnp.zeros((tp_count, group, rows, kind_count, slab_width), jnp.bfloat16)
        for c in range(group):
            perm = []
            for r in range(rep_count):
                for t in range(tp_count):
                    s = group * t + (r - c) % group
                    perm.append((r * tp_count + t, s * tp_count + r // group))
            block = pick(slabs, (rep_index - c) % group, 2)
            got = lax.ppermute(block, ("rep", "tp"), perm)
            spot = (rep_index + c) % group

            def put(buffer, piece, source):
                return lax.dynamic_update_slice(buffer, piece[None, None], (source, spot, 0, 0, 0))

            gathered = put(gathered, got, tp_index)
            for k, passed in enumerate(xor_exchange(lambda k: got, "tp", tp_count), start=1):
                gathered = put(gathered, passed, tp_index ^ k)
        return gathered.reshape(tp_count * group * rows, kind_count, slab_width)

    captured = relayout(jnp.stack([take_rows(lower), take_rows(middle)], axis=1))
    joined = relayout(upper_rows[:, None, :])
    features = jnp.concatenate([captured, joined], axis=1)
    total_rows = features.shape[0]
    feature_flat = features.reshape(total_rows, 3 * slab_width)
    fc_block = fc_weight.reshape(3 * slab_width, fc_weight.shape[2])
    projected = jnp.dot(feature_flat, fc_block, preferred_element_type=jnp.float32)

    by_chip = projected.reshape(chips, 2, rows, projected.shape[1])
    own_parity = pick(by_chip, parity, 1)
    other_parity_rows = pick(by_chip, 1 - parity, 1)

    def sibling_sum(index):
        sent = pick(other_parity_rows, index, 0).astype(jnp.bfloat16)
        got = lax.ppermute(sent, "rep", [(i, i ^ 1) for i in range(rep_count)])
        return pick(own_parity, index, 0) + got.astype(jnp.float32)

    hidden = sibling_sum(chip)
    for k in range(1, chips):
        block = sibling_sum(chip ^ k).astype(jnp.bfloat16)
        got = lax.ppermute(block, "rep", [(i, i ^ (2 * k)) for i in range(rep_count)])
        hidden = hidden + got.astype(jnp.float32)

    scaled = grad_normed.astype(jnp.float32) * norm_gain
    stats = jnp.stack([jnp.sum(hidden * hidden, axis=1), jnp.sum(scaled * hidden, axis=1)])
    step = 1
    while step < tp_count:
        stats = stats + lax.ppermute(stats, "tp", [(i, i ^ step) for i in range(tp_count)])
        step *= 2
    squares, inner_sum = stats[0], stats[1]
    inv_rms = lax.rsqrt(squares / D + EPSILON)
    normed = (hidden * inv_rms[:, None] * norm_gain).astype(jnp.bfloat16)
    hidden_grads = (
        inv_rms[:, None] * scaled - hidden * (inv_rms**3 * inner_sum / D)[:, None]
    ).astype(jnp.bfloat16)

    def to_sibling(piece):
        return lax.ppermute(piece, "rep", [(i, i ^ 1) for i in range(rep_count)])

    empty = jnp.zeros((chips,) + hidden_grads.shape, jnp.bfloat16)
    same_parity = place(empty, hidden_grads, chip)
    other_parity = place(empty, to_sibling(hidden_grads), chip)
    for k in range(1, chips):
        got = lax.ppermute(hidden_grads, "rep", [(i, i ^ (2 * k)) for i in range(rep_count)])
        same_parity = place(same_parity, got, chip ^ k)
        other_parity = place(other_parity, to_sibling(got), chip ^ k)
    both = jnp.zeros((2, chips) + hidden_grads.shape, jnp.bfloat16)
    both = place(place(both, same_parity, parity), other_parity, 1 - parity)
    hidden_grads_all = jnp.swapaxes(both, 0, 1).reshape(rep_count * rows, hidden_grads.shape[1])

    grad_fc = lax.dot_general(
        feature_flat, hidden_grads_all, (((0,), (0,)), ((), ())), preferred_element_type=jnp.float32
    )
    grad_fc = grad_fc.reshape(fc_weight.shape).astype(jnp.bfloat16)
    return (normed, grad_fc)


def solution(mesh):
    in_specs = (
        P("rep", "tp"),
        P("rep", "tp"),
        P("rep", "tp"),
        P("rep", "tp"),
        P("rep"),
        P(None, "rep", "tp"),
        P("tp"),
        P("rep", "tp"),
    )
    out_specs = (P("rep", "tp"), P(None, "rep", "tp"))
    return jax.shard_map(body, mesh=mesh, in_specs=in_specs, out_specs=out_specs, check_vma=False)
```
